1024 devices in a mesh: seq: 64 (over z, core), tp: 16 (over x, y).
Axes of the slice: x: 4, y: 4, z: 32, core: 2. Of those that a mesh axis runs over, the one named last changes fastest.
Arguments:
- lin_query: bfloat16 [8192, 4096], P('seq', 'tp'), may hold values from -23 to 23
- lin_key: bfloat16 [8192, 4096], P('seq', 'tp'), may hold values from -0.5 to 0.5
- lin_value: bfloat16 [8192, 4096], P('seq', 'tp'), may hold values from -6 to 6
- decay_rate: float32 [32], P('tp'), may hold values from 0 to 1
- norm_gain: float32 [4096], P('tp'), may hold values from 0.1 to 1.9
- lin_grad: bfloat16 [8192, 4096], P('seq', 'tp'), may hold values from -6 to 6
- soft_query: bfloat16 [8192, 4096], P('seq', 'tp'), may hold values from -5 to 5
- soft_key: bfloat16 [8192, 4096], P('seq', 'tp'), may hold values from -5 to 5
- soft_value: bfloat16 [8192, 4096], P('seq', 'tp'), may hold values from -6 to 6
- soft_grad: bfloat16 [8192, 4096], P('seq', 'tp'), may hold values from -6 to 6
- segments: int32 [64], replicated, may hold values from 0 to 21, never falling along the last dimension, each value on 1 to 6 neighbouring positions
Outputs:
- lin_query_grad: bfloat16 [8192, 4096], P('seq', 'tp')
- lin_key_grad: bfloat16 [8192, 4096], P('seq', 'tp')
- lin_value_grad: bfloat16 [8192, 4096], P('seq', 'tp')
- soft_query_grad: bfloat16 [8192, 4096], P('seq', 'tp')
- soft_key_grad: bfloat16 [8192, 4096], P('seq', 'tp')
- soft_value_grad: bfloat16 [8192, 4096], P('seq', 'tp')
The draws below stay inside these ranges and needn't reach their ends.
Inputs may be any that keep to these rules, and one draw needn't show every extreme that they name: `segments`: block labels never fall, start at 0, and one label covers at most 6 blocks.
All inputs are finite; a program needn't handle non-finite values.
Results may differ from the reference program's by a relative error of at most 0.013.
Values may be sent and summed in bfloat16 or wider, within the bound.
No kernel may reach another device: no remote copies, remote signals or barrier semaphores. Data moves between devices by JAX's collectives and lax.ppermute only.
A program may use at most 64 MiB of HBM per device.

```python
import math
import jax
import jax.numpy as jnp
import numpy as np
from jax import lax

HD = 128
TOK_DEV = 128
BLK = 128
REACH = 6
HEADS = 32
FEAT = 4096
TOKENS = 8192
NBLK = 64
MOST = 6
DOCS = 22
N_SEQ = 64


def head_ramp(top):
    place = jnp.arange(HEADS).astype(jnp.float32)
    return jnp.repeat(top ** (place / max(HEADS - 1, 1)), HD)


def drawn_rows(key):
    return jnp.clip(jax.random.normal(key, (TOKENS, FEAT), jnp.float32), -4.5, 4.5)


def draw_lin_query(key, part):
    base = drawn_rows(jax.random.fold_in(key, 5))
    ramp = head_ramp(1.8)
    return (base * ramp[None, :]).astype(jnp.bfloat16)


def draw_decay_rate(key, part):
    chain = float(MOST * BLK)
    slow = jnp.exp(jax.random.uniform(jax.random.fold_in(key, 1), (HEADS,), jnp.float32, math.log(0.15 / chain), math.log(2.3 / chain)))
    fast = jax.random.uniform(jax.random.fold_in(key, 2), (HEADS,), jnp.float32, 1.0 / 50.0, 1.0 / 30.0)
    share = 0.5
    pick = jax.random.uniform(jax.random.fold_in(key, 3), (HEADS,), jnp.float32) < share
    return jnp.where(pick, slow, fast).astype(jnp.float32)


def draw_soft_query(key, part):
    base = drawn_rows(jax.random.fold_in(key, 1))
    return base.astype(jnp.bfloat16)


def draw_soft_key(key, part):
    base = drawn_rows(jax.random.fold_in(key, 2))
    return base.astype(jnp.bfloat16)


def levels(stream_key, shape, split, least, largest):
    def one(position, parts):
        heights = jax.random.uniform(jax.random.fold_in(jax.random.fold_in(stream_key, 6), position), (parts,), jnp.float32, least / len(split), largest / len(split))
        return jnp.repeat(jnp.exp(heights), shape[position] // parts).reshape((-1,) + (1,) * (len(shape) - position - 1))

    gain = one(*split[0])
    for cut in split[1:]:
        gain = gain * one(*cut)
    return gain


def length_profile(number_of, total, bound, lean):
    portions = [(1 << 20) // math.isqrt(grade ** lean) + 1 for grade in range(2, number_of + 1)]
    surplus, holding = total - bound - (number_of - 1), [1] * (number_of - 1)
    while surplus > 0:
        free = [i for i in range(number_of - 1) if holding[i] < bound]
        pool, budget = sum([portions[i] for i in free]), surplus
        for i in free:
            more = min(bound - holding[i], max(1, budget * portions[i] // pool), surplus)
            holding[i] = holding[i] + more
            surplus = surplus - more
    return np.array([bound] + holding)


def uneven_parts(stream_key, count, total, reach, slope):
    if count == 2:
        one = jax.random.randint(stream_key, (), max(1, total - reach), min(reach, total - 1) + 1)
        return jnp.stack([one, total - one])
    lengths = jnp.asarray(length_profile(count, total, reach, slope), jnp.int32)
    couples = (count - 1) // 2
    source_of, taker = lengths[1:1 + 2 * couples:2], lengths[2:2 + 2 * couples:2]
    room = jnp.minimum(source_of - 1, reach - taker)
    moved = jax.random.randint(jax.random.fold_in(stream_key, 1), (couples,), 0, 1 << 20) % (room + 1)
    lengths = lengths.at[1:1 + 2 * couples:2].set(source_of - moved).at[2:2 + 2 * couples:2].set(taker + moved)
    return lengths[jax.random.permutation(jax.random.fold_in(stream_key, 2), count)]


def centred(key, extent, width, most, split=(), kind=jnp.bfloat16):
    values = jax.random.normal(key, extent, jnp.float32) * width
    if len(split) > 0:
        values = levels(key, extent, split, -0.22, 0.18) * values
    return jnp.clip(values, min=-most, max=most).astype(kind)


def setup_inputs(seed: int = 0) -> dict:
    streams_of = jax.random.split(jax.random.key(seed), 12)
    return {
        "lin_query": draw_lin_query(jax.random.fold_in(streams_of[11], 71), 0),
        "lin_key": centred(streams_of[1], (TOKENS, FEAT), HD ** -0.5, 0.5, ((0, 64), (1, 16))),
        "lin_value": centred(streams_of[2], (TOKENS, FEAT), 1.0, 6.0, ((0, 64), (1, 16))),
        "decay_rate": draw_decay_rate(jax.random.fold_in(streams_of[11], 71), 0),
        "norm_gain": jnp.clip(1.0 + 0.18 * jax.random.normal(streams_of[4], (FEAT,), jnp.float32), 0.1, 1.9),
        "lin_grad": centred(streams_of[5], (TOKENS, FEAT), 1.0, 6.0, ((0, 64), (1, 16))),
        "soft_query": draw_soft_query(jax.random.fold_in(streams_of[11], 71), 0),
        "soft_key": draw_soft_key(jax.random.fold_in(streams_of[11], 71), 0),
        "soft_value": centred(streams_of[8], (TOKENS, FEAT), 1.0, 6.0, ((0, 64), (1, 16))),
        "soft_grad": centred(streams_of[9], (TOKENS, FEAT), 1.0, 6.0, ((0, 64), (1, 16))),
        "segments": jnp.searchsorted(jnp.cumsum(uneven_parts(streams_of[10], DOCS, NBLK, MOST, 0)), jnp.arange(NBLK), side="right").astype(jnp.int32),
    }


HIGH_PRECISION = lax.Precision.HIGHEST
NORM_EPS = 1e-06

def as_float(array):
    return array.astype(jnp.float32)

def decay_matrix(labels, decay_rate):
    place = jnp.arange(labels.shape[0], dtype=jnp.int32)
    distance = as_float(place[:, None] - place[None, :])
    visible = (labels[:, None] == labels[None, :]) & (distance >= 0)
    return jnp.where(visible[None], jnp.exp(-decay_rate[:, None, None] * jnp.maximum(distance, 0.0)[None]), 0.0)

def entry_weights(labels, decay_rate):
    place = as_float(jnp.arange(labels.shape[0], dtype=jnp.int32))
    return jnp.where((labels == labels[0])[None, :], jnp.exp(-decay_rate[:, None] * place[None, :]), 0.0)

def exit_weights(labels, decay_rate):
    count = labels.shape[0]
    place = as_float(jnp.arange(count, dtype=jnp.int32))
    return jnp.where((labels == labels[-1])[None, :], jnp.exp(-decay_rate[:, None] * (count - 1 - place)[None, :]), 0.0)

def forward_element(keys, values, labels, next_label, decay_rate):
    count = labels.shape[0]
    place = as_float(jnp.arange(count, dtype=jnp.int32))
    link = labels[-1] == next_label
    weight = jnp.where((labels == labels[-1])[None, :] & link, jnp.exp(-decay_rate[:, None] * (count - place)[None, :]), 0.0)
    summary = jnp.einsum('thd,the->hde', as_float(keys) * weight.T[:, :, None], as_float(values), precision=HIGH_PRECISION)
    factor = jnp.where(labels[0] == next_label, jnp.exp(-decay_rate * count), 0.0)
    return (factor, summary)

def backward_element(queries, grads, labels, prev_label, decay_rate):
    count = labels.shape[0]
    place = as_float(jnp.arange(count, dtype=jnp.int32))
    link = labels[0] == prev_label
    weight = jnp.where((labels == labels[0])[None, :] & link, jnp.exp(-decay_rate[:, None] * (place + 1.0)[None, :]), 0.0)
    summary = jnp.einsum('thd,the->hde', as_float(queries) * weight.T[:, :, None], as_float(grads), precision=HIGH_PRECISION)
    factor = jnp.where(link & (labels[0] == labels[-1]), jnp.exp(-decay_rate * count), 0.0)
    return (factor, summary)

def lightning_reference(queries, keys, values, decay_rate, norm_gain, lin_grad, token_labels):
    shape = (N_SEQ, TOK_DEV, HEADS, HD)
    query_spans = queries.reshape(shape)
    key_spans = keys.reshape(shape)
    value_spans = values.reshape(shape)
    labels = token_labels.reshape(N_SEQ, TOK_DEV)
    firsts = labels[:, 0]
    lasts = labels[:, -1]
    nexts = jnp.concatenate([firsts[1:], jnp.full((1,), -2, jnp.int32)])
    prevs = jnp.concatenate([jnp.full((1,), -1, jnp.int32), lasts[:-1]])

    def forward(state, inputs):
        span_query, span_key, span_value, span_labels, next_label = inputs
        decay = decay_matrix(span_labels, decay_rate)
        scores = jnp.einsum('thd,shd->hts', as_float(span_query), as_float(span_key))
        weights = (decay * scores).astype(jnp.bfloat16)
        inner = jnp.einsum('hts,shd->thd', as_float(weights), as_float(span_value))
        entry = entry_weights(span_labels, decay_rate)
        carried = jnp.einsum('thd,hde->the', as_float(span_query), state, precision=HIGH_PRECISION)
        output = inner + carried * entry.T[:, :, None]
        factor, summary = forward_element(span_key, span_value, span_labels, next_label, decay_rate)
        return (summary + factor[:, None, None] * state, (output, state))
    start_state = jnp.zeros((HEADS, HD, HD), jnp.float32)
    _, (outputs, states) = lax.scan(forward, start_state, (query_spans, key_spans, value_spans, labels, nexts))
    flat = outputs.reshape(TOKENS, FEAT)
    scaled_grad = norm_gain[None, :] * as_float(lin_grad)
    mean_square = lax.optimization_barrier(jnp.mean(flat * flat, axis=1))
    cross = lax.optimization_barrier(jnp.mean(flat * scaled_grad, axis=1))
    inverse = lax.rsqrt(mean_square + NORM_EPS)
    norm_grad = (inverse[:, None] * scaled_grad - flat * (inverse ** 3 * cross)[:, None]).astype(jnp.bfloat16)
    grad_spans = norm_grad.reshape(shape)

    def backward(reverse_in, inputs):
        span_query, span_key, span_value, span_grad, span_labels, prev_label, state = inputs
        decay = decay_matrix(span_labels, decay_rate)
        scores = jnp.einsum('thd,shd->hts', as_float(span_query), as_float(span_key))
        weights = (decay * scores).astype(jnp.bfloat16)
        grad_scores = jnp.einsum('thd,shd->hts', as_float(span_grad), as_float(span_value))
        grad_weights = (decay * grad_scores).astype(jnp.bfloat16)
        entry = entry_weights(span_labels, decay_rate)
        leave = exit_weights(span_labels, decay_rate)
        grad_query = jnp.einsum('hts,shd->thd', as_float(grad_weights), as_float(span_key))
        grad_query = grad_query + jnp.einsum('the,hde->thd', as_float(span_grad), state, precision=HIGH_PRECISION) * entry.T[:, :, None]
        grad_key = jnp.einsum('hts,thd->shd', as_float(grad_weights), as_float(span_query))
        grad_key = grad_key + jnp.einsum('she,hde->shd', as_float(span_value), reverse_in, precision=HIGH_PRECISION) * leave.T[:, :, None]
        grad_value = jnp.einsum('hts,the->she', as_float(weights), as_float(span_grad))
        grad_value = grad_value + jnp.einsum('shd,hde->she', as_float(span_key), reverse_in, precision=HIGH_PRECISION) * leave.T[:, :, None]
        factor, summary = backward_element(span_query, span_grad, span_labels, prev_label, decay_rate)
        return (summary + factor[:, None, None] * reverse_in, (grad_query, grad_key, grad_value))
    _, (grad_query, grad_key, grad_value) = lax.scan(backward, start_state, (query_spans, key_spans, value_spans, grad_spans, labels, prevs, states), reverse=True)
    return (grad_query.reshape(TOKENS, FEAT).astype(jnp.bfloat16), grad_key.reshape(TOKENS, FEAT).astype(jnp.bfloat16), grad_value.reshape(TOKENS, FEAT).astype(jnp.bfloat16))

def softmax_reference(queries, keys, values, grads, token_labels):
    scale = 1.0 / math.sqrt(HD)
    margin = (REACH - 1) * TOK_DEV
    query_heads = queries.reshape(TOKENS, HEADS, HD)
    grad_heads = grads.reshape(TOKENS, HEADS, HD)
    key_pad = jnp.concatenate([jnp.zeros((margin, HEADS, HD), jnp.bfloat16), keys.reshape(TOKENS, HEADS, HD)], 0)
    value_pad = jnp.concatenate([jnp.zeros((margin, HEADS, HD), jnp.bfloat16), values.reshape(TOKENS, HEADS, HD)], 0)
    label_pad = jnp.concatenate([jnp.full((margin,), -1, jnp.int32), token_labels], 0)
    query_place = jnp.arange(TOK_DEV, dtype=jnp.int32)
    key_place = jnp.arange(REACH * TOK_DEV, dtype=jnp.int32) - margin

    def step(carry, index):
        grad_keys, grad_values = carry
        start = (index * TOK_DEV).astype(jnp.int32)
        span_query = lax.dynamic_slice_in_dim(query_heads, start, TOK_DEV)
        span_grad = lax.dynamic_slice_in_dim(grad_heads, start, TOK_DEV)
        span_labels = lax.dynamic_slice_in_dim(token_labels, start, TOK_DEV)
        key_window = lax.dynamic_slice_in_dim(key_pad, start, REACH * TOK_DEV)
        value_window = lax.dynamic_slice_in_dim(value_pad, start, REACH * TOK_DEV)
        key_labels = lax.dynamic_slice_in_dim(label_pad, start, REACH * TOK_DEV)
        visible = (key_labels[None, :] == span_labels[:, None]) & (key_place[None, :] <= query_place[:, None])
        scores = jnp.einsum('thd,uhd->htu', as_float(span_query), as_float(key_window)) * scale
        scores = jnp.where(visible[None], scores, -jnp.inf)
        top = lax.optimization_barrier(jnp.max(scores, axis=-1))
        expo = jnp.exp(scores - top[..., None])
        total = lax.optimization_barrier(jnp.sum(expo, axis=-1))
        probs = expo / total[..., None]
        probs_half = probs.astype(jnp.bfloat16)
        attended = jnp.einsum('htu,uhd->thd', as_float(probs_half), as_float(value_window))
        delta = lax.optimization_barrier(jnp.sum(as_float(span_grad) * attended, axis=-1))
        grad_probs = jnp.einsum('thd,uhd->htu', as_float(span_grad), as_float(value_window))
        grad_scores = (probs * (grad_probs - delta.T[:, :, None])).astype(jnp.bfloat16)
        grad_query = jnp.einsum('htu,uhd->thd', as_float(grad_scores), as_float(key_window)) * scale
        grad_key = jnp.einsum('htu,thd->uhd', as_float(grad_scores), as_float(span_query)) * scale
        grad_value = jnp.einsum('htu,thd->uhd', as_float(probs_half), as_float(span_grad))
        old_keys = lax.dynamic_slice_in_dim(grad_keys, start, REACH * TOK_DEV)
        old_values = lax.dynamic_slice_in_dim(grad_values, start, REACH * TOK_DEV)
        grad_keys = lax.dynamic_update_slice_in_dim(grad_keys, old_keys + grad_key, start, 0)
        grad_values = lax.dynamic_update_slice_in_dim(grad_values, old_values + grad_value, start, 0)
        return ((grad_keys, grad_values), grad_query.astype(jnp.bfloat16))
    start_grads = jnp.zeros((TOKENS + margin, HEADS, HD), jnp.float32)
    (grad_keys, grad_values), grad_queries = lax.scan(step, (start_grads, start_grads), jnp.arange(N_SEQ, dtype=jnp.int32))
    return (grad_queries.reshape(TOKENS, FEAT), grad_keys[margin:].reshape(TOKENS, FEAT).astype(jnp.bfloat16), grad_values[margin:].reshape(TOKENS, FEAT).astype(jnp.bfloat16))

def reference(lin_query, lin_key, lin_value, decay_rate, norm_gain, lin_grad, soft_query, soft_key, soft_value, soft_grad, segments):
    token_labels = jnp.repeat(segments, BLK, total_repeat_length=TOKENS)
    lin_query_grad, lin_key_grad, lin_value_grad = lightning_reference(lin_query, lin_key, lin_value, decay_rate, norm_gain, lin_grad, token_labels)
    soft_query_grad, soft_key_grad, soft_value_grad = softmax_reference(soft_query, soft_key, soft_value, soft_grad, token_labels)
    return (lin_query_grad, lin_key_grad, lin_value_grad, soft_query_grad, soft_key_grad, soft_value_grad)
```

```python
import math

import jax
import jax.numpy as jnp
from jax import lax
from jax.sharding import PartitionSpec as P

HD = 128
BLK = 128
REACH = 6


HIGH_PRECISION = lax.Precision.HIGHEST
NORM_EPS = 1e-06


def shifted(value, axis, steps):
    count = lax.axis_size(axis)
    first, last = (max(0, -steps), min(count, count - steps))
    return lax.ppermute(value, axis, [(source, source + steps) for source in range(first, last)])


def tp_sum(value, axis):
    count = lax.axis_size(axis)
    if count & (count - 1):
        return lax.psum(value, axis)
    step = 1
    while step < count:
        value = value + lax.ppermute(value, axis, [(i, i ^ step) for i in range(count)])
        step *= 2
    return value


def packed(*parts):
    return jnp.concatenate([part.reshape(-1) for part in parts])


def unpacked(flat, shapes):
    out, at = [], 0
    for shape in shapes:
        size = math.prod(shape)
        out.append(flat[at : at + size].reshape(shape))
        at += size
    return out


def as_float(array):
    return array.astype(jnp.float32)


def decay_matrix(labels, decay_rate):
    place = jnp.arange(labels.shape[0], dtype=jnp.int32)
    distance = as_float(place[:, None] - place[None, :])
    visible = (labels[:, None] == labels[None, :]) & (distance >= 0)
    return jnp.where(
        visible[None], jnp.exp(-decay_rate[:, None, None] * jnp.maximum(distance, 0.0)[None]), 0.0
    )


def entry_weights(labels, decay_rate):
    place = as_float(jnp.arange(labels.shape[0], dtype=jnp.int32))
    return jnp.where(
        (labels == labels[0])[None, :], jnp.exp(-decay_rate[:, None] * place[None, :]), 0.0
    )


def exit_weights(labels, decay_rate):
    count = labels.shape[0]
    place = as_float(jnp.arange(count, dtype=jnp.int32))
    return jnp.where(
        (labels == labels[-1])[None, :],
        jnp.exp(-decay_rate[:, None] * (count - 1 - place)[None, :]),
        0.0,
    )


def forward_element(keys, values, labels, next_label, decay_rate):
    count = labels.shape[0]
    place = as_float(jnp.arange(count, dtype=jnp.int32))
    link = labels[-1] == next_label
    weight = jnp.where(
        (labels == labels[-1])[None, :] & link,
        jnp.exp(-decay_rate[:, None] * (count - place)[None, :]),
        0.0,
    )
    summary = jnp.einsum(
        "thd,the->hde",
        as_float(keys) * weight.T[:, :, None],
        as_float(values),
        precision=HIGH_PRECISION,
    )
    factor = jnp.where(labels[0] == next_label, jnp.exp(-decay_rate * count), 0.0)
    return (factor, summary)


def backward_element(queries, grads, labels, prev_label, decay_rate):
    count = labels.shape[0]
    place = as_float(jnp.arange(count, dtype=jnp.int32))
    link = labels[0] == prev_label
    weight = jnp.where(
        (labels == labels[0])[None, :] & link,
        jnp.exp(-decay_rate[:, None] * (place + 1.0)[None, :]),
        0.0,
    )
    summary = jnp.einsum(
        "thd,the->hde",
        as_float(queries) * weight.T[:, :, None],
        as_float(grads),
        precision=HIGH_PRECISION,
    )
    factor = jnp.where(link & (labels[0] == labels[-1]), jnp.exp(-decay_rate * count), 0.0)
    return (factor, summary)


def score_grads(probs, grads, value_part, delta):
    grad_probs = jnp.einsum("thd,uhd->htu", grads, value_part, preferred_element_type=jnp.float32)
    return (probs * (grad_probs - delta.T[:, :, None])).astype(jnp.bfloat16)


def body(
    lin_query,
    lin_key,
    lin_value,
    decay_rate,
    norm_gain,
    lin_grad,
    soft_query,
    soft_key,
    soft_value,
    soft_grad,
    segments,
):
    tokens = lin_query.shape[0]
    heads = lin_query.shape[1] // HD
    scale = 1.0 / math.sqrt(HD)
    device = lax.axis_index("seq")
    blocks_each = tokens // BLK
    pad_blocks = REACH * blocks_each
    padded = jnp.concatenate(
        [jnp.full((pad_blocks,), -1, jnp.int32), segments, jnp.full((pad_blocks,), -2, jnp.int32)]
    )
    window_blocks = lax.dynamic_slice_in_dim(
        padded, device * blocks_each, (2 * REACH + 1) * blocks_each
    )
    window_labels = jnp.repeat(window_blocks, BLK, total_repeat_length=(2 * REACH + 1) * tokens)
    own_labels = window_labels[REACH * tokens : (REACH + 1) * tokens]
    prev_label = window_labels[REACH * tokens - 1]
    next_label = window_labels[(REACH + 1) * tokens]
    key_labels = window_labels[tokens : (REACH + 1) * tokens]

    def split_heads(array):
        return array.reshape(tokens, heads, HD)

    queries = split_heads(lin_query)
    keys = split_heads(lin_key)
    values = split_heads(lin_value)
    soft_queries = split_heads(soft_query)
    soft_keys = split_heads(soft_key)
    soft_values = split_heads(soft_value)
    soft_grads = split_heads(soft_grad)
    _, summary = forward_element(keys, values, own_labels, next_label, decay_rate)
    span = 2 * REACH + 1
    firsts = window_blocks[::blocks_each]
    lasts = window_blocks[blocks_each - 1 :: blocks_each]
    full_decay = jnp.exp(-decay_rate * tokens)
    ahead = [
        jnp.where(firsts[at] == firsts[at + 1], full_decay, 0.0) for at in range(span - 1)
    ]
    behind = [None] + [
        jnp.where((firsts[at] == lasts[at - 1]) & (firsts[at] == lasts[at]), full_decay, 0.0)
        for at in range(1, span)
    ]
    kv_shape = soft_keys.shape
    state_shape = summary.shape
    forward_pack = packed(soft_keys, soft_values, summary.astype(jnp.bfloat16))
    received = []
    state_in = jnp.zeros_like(summary)
    chain = jnp.ones_like(decay_rate)
    for back in range(1, REACH):
        got_key, got_value, got_state = unpacked(
            shifted(forward_pack, "seq", back), (kv_shape, kv_shape, state_shape)
        )
        received.append((got_key, got_value))
        state_in = state_in + chain[:, None, None] * as_float(got_state)
        chain = chain * ahead[REACH - back]
    decay = decay_matrix(own_labels, decay_rate)
    scores = jnp.einsum("thd,shd->hts", queries, keys, preferred_element_type=jnp.float32)
    weights = (decay * scores).astype(jnp.bfloat16)
    entry = entry_weights(own_labels, decay_rate)
    leave = exit_weights(own_labels, decay_rate)
    inner = jnp.einsum("hts,shd->thd", weights, values, preferred_element_type=jnp.float32)
    carried = jnp.einsum("thd,hde->the", as_float(queries), state_in, precision=HIGH_PRECISION)
    lin_out = inner + carried * entry.T[:, :, None]
    flat = lin_out.reshape(tokens, heads * HD)
    scaled_grad = norm_gain[None, :] * as_float(lin_grad)
    sums = tp_sum(jnp.stack([jnp.sum(flat * flat, axis=1), jnp.sum(flat * scaled_grad, axis=1)]), "tp")
    width = lax.axis_size("tp") * heads * HD
    inverse = lax.rsqrt(sums[0] / width + NORM_EPS)
    cross = sums[1] / width
    norm_grad = (inverse[:, None] * scaled_grad - flat * (inverse**3 * cross)[:, None]).astype(
        jnp.bfloat16
    )
    grad_heads = split_heads(norm_grad)
    _, back_summary = backward_element(queries, grad_heads, own_labels, prev_label, decay_rate)
    back_state = back_summary.astype(jnp.bfloat16)
    grad_scores_lin = jnp.einsum(
        "thd,shd->hts", grad_heads, values, preferred_element_type=jnp.float32
    )
    grad_weights = (decay * grad_scores_lin).astype(jnp.bfloat16)
    lin_query_grad = jnp.einsum(
        "hts,shd->thd", grad_weights, keys, preferred_element_type=jnp.float32
    )
    lin_query_grad = (
        lin_query_grad
        + jnp.einsum("the,hde->thd", as_float(grad_heads), state_in, precision=HIGH_PRECISION)
        * entry.T[:, :, None]
    )
    lin_key_grad = jnp.einsum(
        "hts,thd->shd", grad_weights, queries, preferred_element_type=jnp.float32
    )

    lin_value_grad = jnp.einsum(
        "hts,the->she", weights, grad_heads, preferred_element_type=jnp.float32
    )

    key_window = jnp.concatenate(
        [received[back - 1][0] for back in range(REACH - 1, 0, -1)] + [soft_keys], 0
    )
    value_window = jnp.concatenate(
        [received[back - 1][1] for back in range(REACH - 1, 0, -1)] + [soft_values], 0
    )
    query_place = jnp.arange(tokens, dtype=jnp.int32)
    key_place = jnp.arange(REACH * tokens, dtype=jnp.int32) - (REACH - 1) * tokens
    visible = (key_labels[None, :] == own_labels[:, None]) & (
        key_place[None, :] <= query_place[:, None]
    )
    soft_scores = (
        jnp.einsum("thd,uhd->htu", soft_queries, key_window, preferred_element_type=jnp.float32)
        * scale
    )
    soft_scores = jnp.where(visible[None], soft_scores, -jnp.inf)
    top = jnp.max(soft_scores, axis=-1)
    expo = jnp.exp(soft_scores - top[..., None])
    total = jnp.sum(expo, axis=-1)
    probs = expo / total[..., None]
    probs_half = probs.astype(jnp.bfloat16)
    attended = jnp.einsum(
        "htu,uhd->thd", probs_half, value_window, preferred_element_type=jnp.float32
    )
    delta = jnp.sum(as_float(soft_grads) * attended, axis=-1)
    grad_scores = score_grads(probs, soft_grads, value_window, delta)
    soft_query_grad = (
        jnp.einsum("htu,uhd->thd", grad_scores, key_window, preferred_element_type=jnp.float32)
        * scale
    )
    key_terms = (
        jnp.einsum("htu,thd->uhd", grad_scores, soft_queries, preferred_element_type=jnp.float32)
        * scale
    )
    value_terms = jnp.einsum(
        "htu,thd->uhd", probs_half, soft_grads, preferred_element_type=jnp.float32
    )
    soft_key_grad = key_terms[(REACH - 1) * tokens :]
    soft_value_grad = value_terms[(REACH - 1) * tokens :]
    reverse_in = jnp.zeros_like(back_summary)
    chain = jnp.ones_like(decay_rate)
    for back in range(1, REACH):
        lower = (REACH - 1 - back) * tokens
        backward_pack = packed(
            key_terms[lower : lower + tokens].astype(jnp.bfloat16),
            value_terms[lower : lower + tokens].astype(jnp.bfloat16),
            back_state,
        )
        got_key, got_value, got_state = unpacked(
            shifted(backward_pack, "seq", -back), (kv_shape, kv_shape, state_shape)
        )
        soft_key_grad = soft_key_grad + as_float(got_key)
        soft_value_grad = soft_value_grad + as_float(got_value)
        reverse_in = reverse_in + chain[:, None, None] * as_float(got_state)
        chain = chain * behind[REACH + back]
    lin_key_grad = lin_key_grad + (
        jnp.einsum("she,hde->shd", as_float(values), reverse_in, precision=HIGH_PRECISION)
        * leave.T[:, :, None]
    )
    lin_value_grad = lin_value_grad + (
        jnp.einsum("shd,hde->she", as_float(keys), reverse_in, precision=HIGH_PRECISION)
        * leave.T[:, :, None]
    )

    def merge_heads(array):
        return array.reshape(tokens, heads * HD).astype(jnp.bfloat16)

    return (
        merge_heads(lin_query_grad),
        merge_heads(lin_key_grad),
        merge_heads(lin_value_grad),
        merge_heads(soft_query_grad),
        merge_heads(soft_key_grad),
        merge_heads(soft_value_grad),
    )


def solution(mesh):
    return jax.shard_map(
        body,
        mesh=mesh,
        in_specs=(
            P("seq", "tp"),
            P("seq", "tp"),
            P("seq", "tp"),
            P("tp"),
            P("tp"),
            P("seq", "tp"),
            P("seq", "tp"),
            P("seq", "tp"),
            P("seq", "tp"),
            P("seq", "tp"),
            P(),
        ),
        out_specs=(
            P("seq", "tp"),
            P("seq", "tp"),
            P("seq", "tp"),
            P("seq", "tp"),
            P("seq", "tp"),
            P("seq", "tp"),
        ),
        check_vma=False,
    )
```

```python
import math

import jax
import jax.numpy as jnp
from jax import lax
from jax.sharding import PartitionSpec as P

HD = 128
BLK = 128
REACH = 6


HIGH_PRECISION = lax.Precision.HIGHEST
NORM_EPS = 1e-06


def shifted(value, axis, steps):
    count = lax.axis_size(axis)
    first, last = (max(0, -steps), min(count, count - steps))
    return lax.ppermute(value, axis, [(source, source + steps) for source in range(first, last)])


def tp_sum(value, axis):
    return jnp.sum(lax.all_gather(value, axis), axis=0)


def packed(*parts):
    return jnp.concatenate([part.reshape(-1) for part in parts])


def unpacked(flat, shapes):
    out, at = [], 0
    for shape in shapes:
        size = math.prod(shape)
        out.append(flat[at : at + size].reshape(shape))
        at += size
    return out


def as_float(array):
    return array.astype(jnp.float32)


def decay_matrix(labels, decay_rate):
    place = jnp.arange(labels.shape[0], dtype=jnp.int32)
    distance = as_float(place[:, None] - place[None, :])
    visible = (labels[:, None] == labels[None, :]) & (distance >= 0)
    return jnp.where(
        visible[None], jnp.exp(-decay_rate[:, None, None] * jnp.maximum(distance, 0.0)[None]), 0.0
    )


def entry_weights(labels, decay_rate):
    place = as_float(jnp.arange(labels.shape[0], dtype=jnp.int32))
    return jnp.where(
        (labels == labels[0])[None, :], jnp.exp(-decay_rate[:, None] * place[None, :]), 0.0
    )


def exit_weights(labels, decay_rate):
    count = labels.shape[0]
    place = as_float(jnp.arange(count, dtype=jnp.int32))
    return jnp.where(
        (labels == labels[-1])[None, :],
        jnp.exp(-decay_rate[:, None] * (count - 1 - place)[None, :]),
        0.0,
    )


def forward_element(keys, values, labels, next_label, decay_rate):
    count = labels.shape[0]
    place = as_float(jnp.arange(count, dtype=jnp.int32))
    link = labels[-1] == next_label
    weight = jnp.where(
        (labels == labels[-1])[None, :] & link,
        jnp.exp(-decay_rate[:, None] * (count - place)[None, :]),
        0.0,
    )
    summary = jnp.einsum(
        "thd,the->hde",
        as_float(keys) * weight.T[:, :, None],
        as_float(values),
        precision=HIGH_PRECISION,
    )
    factor = jnp.where(labels[0] == next_label, jnp.exp(-decay_rate * count), 0.0)
    return (factor, summary)


def backward_element(queries, grads, labels, prev_label, decay_rate):
    count = labels.shape[0]
    place = as_float(jnp.arange(count, dtype=jnp.int32))
    link = labels[0] == prev_label
    weight = jnp.where(
        (labels == labels[0])[None, :] & link,
        jnp.exp(-decay_rate[:, None] * (place + 1.0)[None, :]),
        0.0,
    )
    summary = jnp.einsum(
        "thd,the->hde",
        as_float(queries) * weight.T[:, :, None],
        as_float(grads),
        precision=HIGH_PRECISION,
    )
    factor = jnp.where(link & (labels[0] == labels[-1]), jnp.exp(-decay_rate * count), 0.0)
    return (factor, summary)


def score_grads(probs, grads, value_part, delta):
    grad_probs = jnp.einsum("thd,uhd->htu", grads, value_part, preferred_element_type=jnp.float32)
    return (probs * (grad_probs - delta.T[:, :, None])).astype(jnp.bfloat16)


def body(
    lin_query,
    lin_key,
    lin_value,
    decay_rate,
    norm_gain,
    lin_grad,
    soft_query,
    soft_key,
    soft_value,
    soft_grad,
    segments,
):
    tokens = lin_query.shape[0]
    heads = lin_query.shape[1] // HD
    scale = 1.0 / math.sqrt(HD)
    device = lax.axis_index("seq")
    blocks_each = tokens // BLK
    pad_blocks = REACH * blocks_each
    padded = jnp.concatenate(
        [jnp.full((pad_blocks,), -1, jnp.int32), segments, jnp.full((pad_blocks,), -2, jnp.int32)]
    )
    window_blocks = lax.dynamic_slice_in_dim(
        padded, device * blocks_each, (2 * REACH + 1) * blocks_each
    )
    window_labels = jnp.broadcast_to(window_blocks[:, None], (window_blocks.shape[0], BLK)).reshape(-1)
    own_labels = window_labels[REACH * tokens : (REACH + 1) * tokens]
    prev_label = window_labels[REACH * tokens - 1]
    next_label = window_labels[(REACH + 1) * tokens]
    key_labels = window_labels[tokens : (REACH + 1) * tokens]

    def split_heads(array):
        return array.reshape(tokens, heads, HD)

    queries = split_heads(lin_query)
    keys = split_heads(lin_key)
    values = split_heads(lin_value)
    soft_queries = split_heads(soft_query)
    soft_keys = split_heads(soft_key)
    soft_values = split_heads(soft_value)
    soft_grads = split_heads(soft_grad)
    _, summary = forward_element(keys, values, own_labels, next_label, decay_rate)
    span = 2 * REACH + 1
    firsts = window_blocks[::blocks_each]
    lasts = window_blocks[blocks_each - 1 :: blocks_each]
    full_decay = jnp.exp(-decay_rate * tokens)
    ahead = [
        jnp.where(firsts[at] == firsts[at + 1], full_decay, 0.0) for at in range(span - 1)
    ]
    behind = [None] + [
        jnp.where((firsts[at] == lasts[at - 1]) & (firsts[at] == lasts[at]), full_decay, 0.0)
        for at in range(1, span)
    ]
    kv_shape = soft_keys.shape
    state_shape = summary.shape
    forward_pack = packed(soft_keys, soft_values, summary.astype(jnp.bfloat16))
    received = []
    state_in = jnp.zeros_like(summary)
    chain = jnp.ones_like(decay_rate)
    for back in range(1, REACH):
        got_key, got_value, got_state = unpacked(
            shifted(forward_pack, "seq", back), (kv_shape, kv_shape, state_shape)
        )
        received.append((got_key, got_value))
        state_in = state_in + chain[:, None, None] * as_float(got_state)
        chain = chain * ahead[REACH - back]
    decay = decay_matrix(own_labels, decay_rate)
    scores = jnp.einsum("thd,shd->hts", queries, keys, preferred_element_type=jnp.float32)
    weights = (decay * scores).astype(jnp.bfloat16)
    entry = entry_weights(own_labels, decay_rate)
    leave = exit_weights(own_labels, decay_rate)
    inner = jnp.einsum("hts,shd->thd", weights, values, preferred_element_type=jnp.float32)
    carried = jnp.einsum("thd,hde->the", as_float(queries), state_in, precision=HIGH_PRECISION)
    lin_out = inner + carried * entry.T[:, :, None]
    flat = lin_out.reshape(tokens, heads * HD)
    scaled_grad = norm_gain[None, :] * as_float(lin_grad)
    sums = tp_sum(jnp.stack([jnp.sum(flat * flat, axis=1), jnp.sum(flat * scaled_grad, axis=1)]), "tp")
    width = lax.axis_size("tp") * heads * HD
    inverse = lax.rsqrt(sums[0] / width + NORM_EPS)
    cross = sums[1] / width
    norm_grad = (inverse[:, None] * scaled_grad - flat * (inverse**3 * cross)[:, None]).astype(
        jnp.bfloat16
    )
    grad_heads = split_heads(norm_grad)
    _, back_summary = backward_element(queries, grad_heads, own_labels, prev_label, decay_rate)
    back_state = back_summary.astype(jnp.bfloat16)
    grad_scores_lin = jnp.einsum(
        "thd,shd->hts", grad_heads, values, preferred_element_type=jnp.float32
    )
    grad_weights = (decay * grad_scores_lin).astype(jnp.bfloat16)
    lin_query_grad = jnp.einsum(
        "hts,shd->thd", grad_weights, keys, preferred_element_type=jnp.float32
    )
    lin_query_grad = (
        lin_query_grad
        + jnp.einsum("the,hde->thd", as_float(grad_heads), state_in, precision=HIGH_PRECISION)
        * entry.T[:, :, None]
    )
    lin_key_grad = jnp.einsum(
        "hts,thd->shd", grad_weights, queries, preferred_element_type=jnp.float32
    )

    lin_value_grad = jnp.einsum(
        "hts,the->she", weights, grad_heads, preferred_element_type=jnp.float32
    )

    key_window = jnp.concatenate(
        [received[back - 1][0] for back in range(REACH - 1, 0, -1)] + [soft_keys], 0
    )
    value_window = jnp.concatenate(
        [received[back - 1][1] for back in range(REACH - 1, 0, -1)] + [soft_values], 0
    )
    query_place = jnp.arange(tokens, dtype=jnp.int32)
    key_place = jnp.arange(REACH * tokens, dtype=jnp.int32) - (REACH - 1) * tokens
    visible = (key_labels[None, :] == own_labels[:, None]) & (
        key_place[None, :] <= query_place[:, None]
    )
    soft_scores = (
        jnp.einsum("thd,uhd->htu", soft_queries, key_window, preferred_element_type=jnp.float32)
        * scale
    )
    soft_scores = jnp.where(visible[None], soft_scores, -jnp.inf)
    top = jnp.max(soft_scores, axis=-1)
    expo = jnp.exp(soft_scores - top[..., None])
    total = jnp.sum(expo, axis=-1)
    probs = expo / total[..., None]
    probs_half = probs.astype(jnp.bfloat16)
    attended = jnp.einsum(
        "htu,uhd->thd", probs_half, value_window, preferred_element_type=jnp.float32
    )
    delta = jnp.sum(as_float(soft_grads) * attended, axis=-1)
    grad_scores = score_grads(probs, soft_grads, value_window, delta)
    soft_query_grad = (
        jnp.einsum("htu,uhd->thd", grad_scores, key_window, preferred_element_type=jnp.float32)
        * scale
    )
    key_terms = (
        jnp.einsum("htu,thd->uhd", grad_scores, soft_queries, preferred_element_type=jnp.float32)
        * scale
    )
    value_terms = jnp.einsum(
        "htu,thd->uhd", probs_half, soft_grads, preferred_element_type=jnp.float32
    )
    soft_key_grad = key_terms[(REACH - 1) * tokens :]
    soft_value_grad = value_terms[(REACH - 1) * tokens :]
    reverse_in = jnp.zeros_like(back_summary)
    chain = jnp.ones_like(decay_rate)
    for back in range(1, REACH):
        lower = (REACH - 1 - back) * tokens
        backward_pack = packed(
            key_terms[lower : lower + tokens].astype(jnp.bfloat16),
            value_terms[lower : lower + tokens].astype(jnp.bfloat16),
            back_state,
        )
        got_key, got_value, got_state = unpacked(
            shifted(backward_pack, "seq", -back), (kv_shape, kv_shape, state_shape)
        )
        soft_key_grad = soft_key_grad + as_float(got_key)
        soft_value_grad = soft_value_grad + as_float(got_value)
        reverse_in = reverse_in + chain[:, None, None] * as_float(got_state)
        chain = chain * behind[REACH + back]
    lin_key_grad = lin_key_grad + (
        jnp.einsum("she,hde->shd", as_float(values), reverse_in, precision=HIGH_PRECISION)
        * leave.T[:, :, None]
    )
    lin_value_grad = lin_value_grad + (
        jnp.einsum("shd,hde->she", as_float(keys), reverse_in, precision=HIGH_PRECISION)
        * leave.T[:, :, None]
    )

    def merge_heads(array):
        return array.reshape(tokens, heads * HD).astype(jnp.bfloat16)

    return (
        merge_heads(lin_query_grad),
        merge_heads(lin_key_grad),
        merge_heads(lin_value_grad),
        merge_heads(soft_query_grad),
        merge_heads(soft_key_grad),
        merge_heads(soft_value_grad),
    )


def solution(mesh):
    return jax.shard_map(
        body,
        mesh=mesh,
        in_specs=(
            P("seq", "tp"),
            P("seq", "tp"),
            P("seq", "tp"),
            P("tp"),
            P("tp"),
            P("seq", "tp"),
            P("seq", "tp"),
            P("seq", "tp"),
            P("seq", "tp"),
            P("seq", "tp"),
            P(),
        ),
        out_specs=(
            P("seq", "tp"),
            P("seq", "tp"),
            P("seq", "tp"),
            P("seq", "tp"),
            P("seq", "tp"),
            P("seq", "tp"),
        ),
        check_vma=False,
    )
```

```python
import math

import jax
import jax.numpy as jnp
from jax import lax
from jax.sharding import PartitionSpec as P

HD = 128
BLK = 128
REACH = 6


HIGH_PRECISION = lax.Precision.HIGHEST
NORM_EPS = 1e-06


def shifted(value, axis, steps):
    count = lax.axis_size(axis)
    first, last = (max(0, -steps), min(count, count - steps))
    return lax.ppermute(value, axis, [(source, source + steps) for source in range(first, last)])


def tp_sum(value, axis):
    return lax.psum(value, axis)


def packed(*parts):
    return jnp.concatenate([part.reshape(-1) for part in parts])


def unpacked(flat, shapes):
    out, at = [], 0
    for shape in shapes:
        size = math.prod(shape)
        out.append(flat[at : at + size].reshape(shape))
        at += size
    return out


def as_float(array):
    return array.astype(jnp.float32)


def decay_matrix(labels, decay_rate):
    place = jnp.arange(labels.shape[0], dtype=jnp.int32)
    distance = as_float(place[:, None] - place[None, :])
    visible = (labels[:, None] == labels[None, :]) & (distance >= 0)
    return jnp.where(
        visible[None], jnp.exp(-decay_rate[:, None, None] * jnp.maximum(distance, 0.0)[None]), 0.0
    )


def entry_weights(labels, decay_rate):
    place = as_float(jnp.arange(labels.shape[0], dtype=jnp.int32))
    return jnp.where(
        (labels == labels[:1])[None, :], jnp.exp(-decay_rate[:, None] * place[None, :]), 0.0
    )


def exit_weights(labels, decay_rate):
    count = labels.shape[0]
    place = as_float(jnp.arange(count, dtype=jnp.int32))
    return jnp.where(
        (labels == labels[-1:])[None, :],
        jnp.exp(-decay_rate[:, None] * (count - 1 - place)[None, :]),
        0.0,
    )


def forward_summary(keys, values, labels, link, decay_rate):
    count = labels.shape[0]
    place = as_float(jnp.arange(count, dtype=jnp.int32))
    weight = jnp.where(
        (labels == labels[-1:])[None, :] & link[None, :],
        jnp.exp(-decay_rate[:, None] * (count - place)[None, :]),
        0.0,
    )
    return jnp.einsum(
        "thd,the->hde",
        as_float(keys) * weight.T[:, :, None],
        as_float(values),
        precision=HIGH_PRECISION,
    )


def backward_summary(queries, grads, labels, link, decay_rate):
    count = labels.shape[0]
    place = as_float(jnp.arange(count, dtype=jnp.int32))
    weight = jnp.where(
        (labels == labels[:1])[None, :] & link[None, :],
        jnp.exp(-decay_rate[:, None] * (place + 1.0)[None, :]),
        0.0,
    )
    return jnp.einsum(
        "thd,the->hde",
        as_float(queries) * weight.T[:, :, None],
        as_float(grads),
        precision=HIGH_PRECISION,
    )


def score_grads(probs, grads, value_part, delta):
    grad_probs = jnp.einsum("thd,uhd->htu", grads, value_part, preferred_element_type=jnp.float32)
    return (probs * (grad_probs - delta.T[:, :, None])).astype(jnp.bfloat16)


def body(
    lin_query,
    lin_key,
    lin_value,
    decay_rate,
    norm_gain,
    lin_grad,
    soft_query,
    soft_key,
    soft_value,
    soft_grad,
    segments,
):
    tokens = lin_query.shape[0]
    heads = lin_query.shape[1] // HD
    scale = 1.0 / math.sqrt(HD)
    device = lax.axis_index("seq")
    blocks_each = tokens // BLK
    pad_blocks = REACH * blocks_each
    padded = jnp.concatenate(
        [jnp.full((pad_blocks,), -1, jnp.int32), segments, jnp.full((pad_blocks,), -2, jnp.int32)]
    )
    window_blocks = lax.dynamic_slice_in_dim(
        padded, device * blocks_each, (2 * REACH + 1) * blocks_each
    )
    window_labels = jnp.broadcast_to(window_blocks[:, None], (window_blocks.shape[0], BLK)).reshape(-1)
    own_labels = window_labels[REACH * tokens : (REACH + 1) * tokens]
    key_labels = window_labels[tokens : (REACH + 1) * tokens]

    def split_heads(array):
        return array.reshape(tokens, heads, HD)

    queries = split_heads(lin_query)
    keys = split_heads(lin_key)
    values = split_heads(lin_value)
    soft_queries = split_heads(soft_query)
    soft_keys = split_heads(soft_key)
    soft_values = split_heads(soft_value)
    soft_grads = split_heads(soft_grad)
    span = 2 * REACH + 1
    firsts = window_blocks[::blocks_each]
    lasts = window_blocks[blocks_each - 1 :: blocks_each]
    summary = forward_summary(
        keys, values, own_labels, lasts[REACH : REACH + 1] == firsts[REACH + 1 : REACH + 2], decay_rate
    )
    full_decay = jnp.exp(-decay_rate * tokens)
    ahead = jnp.where((firsts[:-1] == firsts[1:])[:, None], full_decay[None, :], 0.0)
    behind = jnp.where(
        ((firsts[1:] == lasts[:-1]) & (firsts[1:] == lasts[1:]))[:, None], full_decay[None, :], 0.0
    )
    kv_shape = soft_keys.shape
    state_shape = summary.shape
    forward_pack = packed(soft_keys, soft_values, summary.astype(jnp.bfloat16))
    received = []
    state_in = jnp.zeros_like(summary)
    for back in range(1, REACH):
        got_key, got_value, got_state = unpacked(
            shifted(forward_pack, "seq", back), (kv_shape, kv_shape, state_shape)
        )
        received.append((got_key, got_value))
        chain = jnp.prod(ahead[REACH - back + 1 : REACH], axis=0)
        state_in = state_in + chain[:, None, None] * as_float(got_state)
    decay = decay_matrix(own_labels, decay_rate)
    scores = jnp.einsum("thd,shd->hts", queries, keys, preferred_element_type=jnp.float32)
    weights = (decay * scores).astype(jnp.bfloat16)
    entry = entry_weights(own_labels, decay_rate)
    leave = exit_weights(own_labels, decay_rate)
    inner = jnp.einsum("hts,shd->thd", weights, values, preferred_element_type=jnp.float32)
    carried = jnp.einsum("thd,hde->the", as_float(queries), state_in, precision=HIGH_PRECISION)
    lin_out = inner + carried * entry.T[:, :, None]
    flat = lin_out.reshape(tokens, heads * HD)
    scaled_grad = norm_gain[None, :] * as_float(lin_grad)
    sums = tp_sum(jnp.stack([jnp.sum(flat * flat, axis=1), jnp.sum(flat * scaled_grad, axis=1)]), "tp")
    width = lax.axis_size("tp") * heads * HD
    inverse = lax.rsqrt(sums[0] / width + NORM_EPS)
    cross = sums[1] / width
    norm_grad = (inverse[:, None] * scaled_grad - flat * (inverse**3 * cross)[:, None]).astype(
        jnp.bfloat16
    )
    grad_heads = split_heads(norm_grad)
    back_summary = backward_summary(
        queries, grad_heads, own_labels, firsts[REACH : REACH + 1] == lasts[REACH - 1 : REACH], decay_rate
    )
    back_state = back_summary.astype(jnp.bfloat16)
    grad_scores_lin = jnp.einsum(
        "thd,shd->hts", grad_heads, values, preferred_element_type=jnp.float32
    )
    grad_weights = (decay * grad_scores_lin).astype(jnp.bfloat16)
    lin_query_grad = jnp.einsum(
        "hts,shd->thd", grad_weights, keys, preferred_element_type=jnp.float32
    )
    lin_query_grad = (
        lin_query_grad
        + jnp.einsum("the,hde->thd", as_float(grad_heads), state_in, precision=HIGH_PRECISION)
        * entry.T[:, :, None]
    )
    lin_key_grad = jnp.einsum(
        "hts,thd->shd", grad_weights, queries, preferred_element_type=jnp.float32
    )

    lin_value_grad = jnp.einsum(
        "hts,the->she", weights, grad_heads, preferred_element_type=jnp.float32
    )

    key_window = jnp.concatenate(
        [received[back - 1][0] for back in range(REACH - 1, 0, -1)] + [soft_keys], 0
    )
    value_window = jnp.concatenate(
        [received[back - 1][1] for back in range(REACH - 1, 0, -1)] + [soft_values], 0
    )
    query_place = jnp.arange(tokens, dtype=jnp.int32)
    key_place = jnp.arange(REACH * tokens, dtype=jnp.int32) - (REACH - 1) * tokens
    visible = (key_labels[None, :] == own_labels[:, None]) & (
        key_place[None, :] <= query_place[:, None]
    )
    soft_scores = (
        jnp.einsum("thd,uhd->htu", soft_queries, key_window, preferred_element_type=jnp.float32)
        * scale
    )
    soft_scores = jnp.where(visible[None], soft_scores, -jnp.inf)
    top = jnp.max(soft_scores, axis=-1)
    expo = jnp.exp(soft_scores - top[..., None])
    total = jnp.sum(expo, axis=-1)
    probs = expo / total[..., None]
    probs_half = probs.astype(jnp.bfloat16)
    attended = jnp.einsum(
        "htu,uhd->thd", probs_half, value_window, preferred_element_type=jnp.float32
    )
    delta = jnp.sum(as_float(soft_grads) * attended, axis=-1)
    grad_scores = score_grads(probs, soft_grads, value_window, delta)
    soft_query_grad = (
        jnp.einsum("htu,uhd->thd", grad_scores, key_window, preferred_element_type=jnp.float32)
        * scale
    )
    key_terms = (
        jnp.einsum("htu,thd->uhd", grad_scores, soft_queries, preferred_element_type=jnp.float32)
        * scale
    )
    value_terms = jnp.einsum(
        "htu,thd->uhd", probs_half, soft_grads, preferred_element_type=jnp.float32
    )
    soft_key_grad = key_terms[(REACH - 1) * tokens :]
    soft_value_grad = value_terms[(REACH - 1) * tokens :]
    reverse_in = jnp.zeros_like(back_summary)
    for back in range(1, REACH):
        lower = (REACH - 1 - back) * tokens
        backward_pack = packed(
            key_terms[lower : lower + tokens].astype(jnp.bfloat16),
            value_terms[lower : lower + tokens].astype(jnp.bfloat16),
            back_state,
        )
        got_key, got_value, got_state = unpacked(
            shifted(backward_pack, "seq", -back), (kv_shape, kv_shape, state_shape)
        )
        soft_key_grad = soft_key_grad + as_float(got_key)
        soft_value_grad = soft_value_grad + as_float(got_value)
        chain = jnp.prod(behind[REACH : REACH + back - 1], axis=0)
        reverse_in = reverse_in + chain[:, None, None] * as_float(got_state)
    lin_key_grad = lin_key_grad + (
        jnp.einsum("she,hde->shd", as_float(values), reverse_in, precision=HIGH_PRECISION)
        * leave.T[:, :, None]
    )
    lin_value_grad = lin_value_grad + (
        jnp.einsum("shd,hde->she", as_float(keys), reverse_in, precision=HIGH_PRECISION)
        * leave.T[:, :, None]
    )

    def merge_heads(array):
        return array.reshape(tokens, heads * HD).astype(jnp.bfloat16)

    return (
        merge_heads(lin_query_grad),
        merge_heads(lin_key_grad),
        merge_heads(lin_value_grad),
        merge_heads(soft_query_grad),
        merge_heads(soft_key_grad),
        merge_heads(soft_value_grad),
    )


def solution(mesh):
    return jax.shard_map(
        body,
        mesh=mesh,
        in_specs=(
            P("seq", "tp"),
            P("seq", "tp"),
            P("seq", "tp"),
            P("tp"),
            P("tp"),
            P("seq", "tp"),
            P("seq", "tp"),
            P("seq", "tp"),
            P("seq", "tp"),
            P("seq", "tp"),
            P(),
        ),
        out_specs=(
            P("seq", "tp"),
            P("seq", "tp"),
            P("seq", "tp"),
            P("seq", "tp"),
            P("seq", "tp"),
            P("seq", "tp"),
        ),
        check_vma=False,
    )
```

```python
import math

import jax
import jax.numpy as jnp
from jax import lax
from jax.sharding import PartitionSpec as P

HD = 128
BLK = 128
REACH = 6


HIGH_PRECISION = lax.Precision.HIGHEST
NORM_EPS = 1e-06


def shifted(value, axis, steps):
    count = lax.axis_size(axis)
    first, last = (max(0, -steps), min(count, count - steps))
    return lax.ppermute(value, axis, [(source, source + steps) for source in range(first, last)])


def tp_sum(value, axis):
    return jnp.sum(lax.all_gather(value, axis), axis=0)


def packed(*parts):
    return jnp.concatenate([part.reshape(-1) for part in parts])


def unpacked(flat, shapes):
    out, at = [], 0
    for shape in shapes:
        size = math.prod(shape)
        out.append(flat[at : at + size].reshape(shape))
        at += size
    return out


def as_float(array):
    return array.astype(jnp.float32)


def decay_matrix(labels, decay_rate):
    place = jnp.arange(labels.shape[0], dtype=jnp.int32)
    distance = as_float(place[:, None] - place[None, :])
    visible = (labels[:, None] == labels[None, :]) & (distance >= 0)
    return jnp.where(
        visible[None], jnp.exp(-decay_rate[:, None, None] * jnp.maximum(distance, 0.0)[None]), 0.0
    )


def entry_weights(labels, decay_rate):
    place = as_float(jnp.arange(labels.shape[0], dtype=jnp.int32))
    return jnp.where(
        (labels == labels[:1])[None, :], jnp.exp(-decay_rate[:, None] * place[None, :]), 0.0
    )


def exit_weights(labels, decay_rate):
    count = labels.shape[0]
    place = as_float(jnp.arange(count, dtype=jnp.int32))
    return jnp.where(
        (labels == labels[-1:])[None, :],
        jnp.exp(-decay_rate[:, None] * (count - 1 - place)[None, :]),
        0.0,
    )


def forward_summary(keys, values, labels, link, decay_rate):
    count = labels.shape[0]
    place = as_float(jnp.arange(count, dtype=jnp.int32))
    weight = jnp.where(
        (labels == labels[-1:])[None, :] & link[None, :],
        jnp.exp(-decay_rate[:, None] * (count - place)[None, :]),
        0.0,
    )
    return jnp.einsum(
        "thd,the->hde",
        as_float(keys) * weight.T[:, :, None],
        as_float(values),
        precision=HIGH_PRECISION,
    )


def backward_summary(queries, grads, labels, link, decay_rate):
    count = labels.shape[0]
    place = as_float(jnp.arange(count, dtype=jnp.int32))
    weight = jnp.where(
        (labels == labels[:1])[None, :] & link[None, :],
        jnp.exp(-decay_rate[:, None] * (place + 1.0)[None, :]),
        0.0,
    )
    return jnp.einsum(
        "thd,the->hde",
        as_float(queries) * weight.T[:, :, None],
        as_float(grads),
        precision=HIGH_PRECISION,
    )


def score_grads(probs, grads, value_part, delta):
    grad_probs = jnp.einsum("thd,uhd->htu", grads, value_part, preferred_element_type=jnp.float32)
    return (probs * (grad_probs - delta.T[:, :, None])).astype(jnp.bfloat16)


def body(
    lin_query,
    lin_key,
    lin_value,
    decay_rate,
    norm_gain,
    lin_grad,
    soft_query,
    soft_key,
    soft_value,
    soft_grad,
    segments,
):
    tokens = lin_query.shape[0]
    heads = lin_query.shape[1] // HD
    scale = 1.0 / math.sqrt(HD)
    device = lax.axis_index("seq")
    blocks_each = tokens // BLK
    pad_blocks = REACH * blocks_each
    padded = jnp.concatenate(
        [jnp.full((pad_blocks,), -1, jnp.int32), segments, jnp.full((pad_blocks,), -2, jnp.int32)]
    )
    window_blocks = lax.dynamic_slice_in_dim(
        padded, device * blocks_each, (2 * REACH + 1) * blocks_each
    )
    window_labels = jnp.broadcast_to(window_blocks[:, None], (window_blocks.shape[0], BLK)).reshape(-1)
    own_labels = window_labels[REACH * tokens : (REACH + 1) * tokens]
    key_labels = window_labels[tokens : (REACH + 1) * tokens]

    def split_heads(array):
        return array.reshape(tokens, heads, HD)

    queries = split_heads(lin_query)
    keys = split_heads(lin_key)
    values = split_heads(lin_value)
    soft_queries = split_heads(soft_query)
    soft_keys = split_heads(soft_key)
    soft_values = split_heads(soft_value)
    soft_grads = split_heads(soft_grad)
    span = 2 * REACH + 1
    firsts = window_blocks[::blocks_each]
    lasts = window_blocks[blocks_each - 1 :: blocks_each]
    summary = forward_summary(
        keys, values, own_labels, lasts[REACH : REACH + 1] == firsts[REACH + 1 : REACH + 2], decay_rate
    )
    full_decay = jnp.exp(-decay_rate * tokens)
    ahead = jnp.where((firsts[:-1] == firsts[1:])[:, None], full_decay[None, :], 0.0)
    behind = jnp.where(
        ((firsts[1:] == lasts[:-1]) & (firsts[1:] == lasts[1:]))[:, None], full_decay[None, :], 0.0
    )
    kv_shape = soft_keys.shape
    state_shape = summary.shape
    unit = packed(soft_keys, soft_values, summary.astype(jnp.bfloat16))
    size = unit.shape[0]
    two_back = shifted(unit, "seq", 2)
    four_back = shifted(two_back, "seq", 2)
    odd_back = shifted(jnp.concatenate([unit, two_back]), "seq", 1)
    five_back = shifted(four_back, "seq", 1)
    arrived = {
        1: odd_back[:size],
        2: two_back,
        3: odd_back[size:],
        4: four_back,
        5: five_back,
    }
    received = []
    state_in = jnp.zeros_like(summary)
    for back in range(1, REACH):
        got_key, got_value, got_state = unpacked(arrived[back], (kv_shape, kv_shape, state_shape))
        received.append((got_key, got_value))
        chain = jnp.prod(ahead[REACH - back + 1 : REACH], axis=0)
        state_in = state_in + chain[:, None, None] * as_float(got_state)
    decay = decay_matrix(own_labels, decay_rate)
    scores = jnp.einsum("thd,shd->hts", queries, keys, preferred_element_type=jnp.float32)
    weights = (decay * scores).astype(jnp.bfloat16)
    entry = entry_weights(own_labels, decay_rate)
    leave = exit_weights(own_labels, decay_rate)
    inner = jnp.einsum("hts,shd->thd", weights, values, preferred_element_type=jnp.float32)
    carried = jnp.einsum("thd,hde->the", as_float(queries), state_in, precision=HIGH_PRECISION)
    lin_out = inner + carried * entry.T[:, :, None]
    flat = lin_out.reshape(tokens, heads * HD)
    scaled_grad = norm_gain[None, :] * as_float(lin_grad)
    sums = tp_sum(jnp.stack([jnp.sum(flat * flat, axis=1), jnp.sum(flat * scaled_grad, axis=1)]), "tp")
    width = lax.axis_size("tp") * heads * HD
    inverse = lax.rsqrt(sums[0] / width + NORM_EPS)
    cross = sums[1] / width
    norm_grad = (inverse[:, None] * scaled_grad - flat * (inverse**3 * cross)[:, None]).astype(
        jnp.bfloat16
    )
    grad_heads = split_heads(norm_grad)
    back_summary = backward_summary(
        queries, grad_heads, own_labels, firsts[REACH : REACH + 1] == lasts[REACH - 1 : REACH], decay_rate
    )
    back_state = back_summary.astype(jnp.bfloat16)
    grad_scores_lin = jnp.einsum(
        "thd,shd->hts", grad_heads, values, preferred_element_type=jnp.float32
    )
    grad_weights = (decay * grad_scores_lin).astype(jnp.bfloat16)
    lin_query_grad = jnp.einsum(
        "hts,shd->thd", grad_weights, keys, preferred_element_type=jnp.float32
    )
    lin_query_grad = (
        lin_query_grad
        + jnp.einsum("the,hde->thd", as_float(grad_heads), state_in, precision=HIGH_PRECISION)
        * entry.T[:, :, None]
    )
    lin_key_grad = jnp.einsum(
        "hts,thd->shd", grad_weights, queries, preferred_element_type=jnp.float32
    )

    lin_value_grad = jnp.einsum(
        "hts,the->she", weights, grad_heads, preferred_element_type=jnp.float32
    )

    key_window = jnp.concatenate(
        [received[back - 1][0] for back in range(REACH - 1, 0, -1)] + [soft_keys], 0
    )
    value_window = jnp.concatenate(
        [received[back - 1][1] for back in range(REACH - 1, 0, -1)] + [soft_values], 0
    )
    query_place = jnp.arange(tokens, dtype=jnp.int32)
    key_place = jnp.arange(REACH * tokens, dtype=jnp.int32) - (REACH - 1) * tokens
    visible = (key_labels[None, :] == own_labels[:, None]) & (
        key_place[None, :] <= query_place[:, None]
    )
    soft_scores = (
        jnp.einsum("thd,uhd->htu", soft_queries, key_window, preferred_element_type=jnp.float32)
        * scale
    )
    soft_scores = jnp.where(visible[None], soft_scores, -jnp.inf)
    top = jnp.max(soft_scores, axis=-1)
    expo = jnp.exp(soft_scores - top[..., None])
    total = jnp.sum(expo, axis=-1)
    probs = expo / total[..., None]
    probs_half = probs.astype(jnp.bfloat16)
    attended = jnp.einsum(
        "htu,uhd->thd", probs_half, value_window, preferred_element_type=jnp.float32
    )
    delta = jnp.sum(as_float(soft_grads) * attended, axis=-1)
    grad_scores = score_grads(probs, soft_grads, value_window, delta)
    soft_query_grad = (
        jnp.einsum("htu,uhd->thd", grad_scores, key_window, preferred_element_type=jnp.float32)
        * scale
    )
    key_terms = (
        jnp.einsum("htu,thd->uhd", grad_scores, soft_queries, preferred_element_type=jnp.float32)
        * scale
    )
    value_terms = jnp.einsum(
        "htu,thd->uhd", probs_half, soft_grads, preferred_element_type=jnp.float32
    )
    soft_key_grad = key_terms[(REACH - 1) * tokens :]
    soft_value_grad = value_terms[(REACH - 1) * tokens :]
    items = {}
    for back in range(1, REACH):
        lower = (REACH - 1 - back) * tokens
        chain = jnp.prod(behind[REACH - back : REACH - 1], axis=0)
        items[back] = packed(
            key_terms[lower : lower + tokens],
            value_terms[lower : lower + tokens],
            chain[:, None, None] * back_summary,
        )
    size = items[1].shape[0]

    def wire(value):
        return value.astype(jnp.bfloat16)

    first = as_float(shifted(wire(jnp.concatenate([items[5], items[3], items[1]])), "seq", -1))
    second = as_float(
        shifted(
            wire(jnp.concatenate([items[2] + first[size : 2 * size], items[4] + first[:size]])),
            "seq",
            -2,
        )
    )
    third = as_float(shifted(wire(second[size:]), "seq", -2))
    total = first[2 * size :] + second[:size] + third
    got_key, got_value, reverse_in = unpacked(total, (kv_shape, kv_shape, state_shape))
    soft_key_grad = soft_key_grad + got_key
    soft_value_grad = soft_value_grad + got_value
    lin_key_grad = lin_key_grad + (
        jnp.einsum("she,hde->shd", as_float(values), reverse_in, precision=HIGH_PRECISION)
        * leave.T[:, :, None]
    )
    lin_value_grad = lin_value_grad + (
        jnp.einsum("shd,hde->she", as_float(keys), reverse_in, precision=HIGH_PRECISION)
        * leave.T[:, :, None]
    )

    def merge_heads(array):
        return array.reshape(tokens, heads * HD).astype(jnp.bfloat16)

    return (
        merge_heads(lin_query_grad),
        merge_heads(lin_key_grad),
        merge_heads(lin_value_grad),
        merge_heads(soft_query_grad),
        merge_heads(soft_key_grad),
        merge_heads(soft_value_grad),
    )


def solution(mesh):
    return jax.shard_map(
        body,
        mesh=mesh,
        in_specs=(
            P("seq", "tp"),
            P("seq", "tp"),
            P("seq", "tp"),
            P("tp"),
            P("tp"),
            P("seq", "tp"),
            P("seq", "tp"),
            P("seq", "tp"),
            P("seq", "tp"),
            P("seq", "tp"),
            P(),
        ),
        out_specs=(
            P("seq", "tp"),
            P("seq", "tp"),
            P("seq", "tp"),
            P("seq", "tp"),
            P("seq", "tp"),
            P("seq", "tp"),
        ),
        check_vma=False,
    )
```

```python
import math

import jax
import jax.numpy as jnp
from jax import lax
from jax.sharding import PartitionSpec as P

HD = 128
BLK = 128
REACH = 6


HIGH_PRECISION = lax.Precision.HIGHEST
NORM_EPS = 1e-06


def shifted(value, axis, steps):
    count = lax.axis_size(axis)
    first, last = (max(0, -steps), min(count, count - steps))
    return lax.ppermute(value, axis, [(source, source + steps) for source in range(first, last)])


def tp_sum(value, axis):
    count = lax.axis_size(axis)
    inner = math.isqrt(count)
    if inner * inner != count:
        return jnp.sum(lax.all_gather(value, axis), axis=0)
    for stride in (1, inner):
        parts = [value]
        for step in range(1, inner):
            pairs = []
            for source in range(count):
                digit = (source // stride) % inner
                target = source + (((digit + step) % inner) - digit) * stride
                pairs.append((source, target))
            parts.append(lax.ppermute(value, axis, pairs))
        value = sum(parts[1:], parts[0])
    return value


def packed(*parts):
    return jnp.concatenate([part.reshape(-1) for part in parts])


def unpacked(flat, shapes):
    out, at = [], 0
    for shape in shapes:
        size = math.prod(shape)
        out.append(flat[at : at + size].reshape(shape))
        at += size
    return out


def as_float(array):
    return array.astype(jnp.float32)


def decay_matrix(labels, decay_rate):
    place = jnp.arange(labels.shape[0], dtype=jnp.int32)
    distance = as_float(place[:, None] - place[None, :])
    visible = (labels[:, None] == labels[None, :]) & (distance >= 0)
    return jnp.where(
        visible[None], jnp.exp(-decay_rate[:, None, None] * jnp.maximum(distance, 0.0)[None]), 0.0
    )


def entry_weights(labels, decay_rate):
    place = as_float(jnp.arange(labels.shape[0], dtype=jnp.int32))
    return jnp.where(
        (labels == labels[:1])[None, :], jnp.exp(-decay_rate[:, None] * place[None, :]), 0.0
    )


def exit_weights(labels, decay_rate):
    count = labels.shape[0]
    place = as_float(jnp.arange(count, dtype=jnp.int32))
    return jnp.where(
        (labels == labels[-1:])[None, :],
        jnp.exp(-decay_rate[:, None] * (count - 1 - place)[None, :]),
        0.0,
    )


def forward_summary(keys, values, labels, link, decay_rate):
    count = labels.shape[0]
    place = as_float(jnp.arange(count, dtype=jnp.int32))
    weight = jnp.where(
        (labels == labels[-1:])[None, :] & link[None, :],
        jnp.exp(-decay_rate[:, None] * (count - place)[None, :]),
        0.0,
    )
    return jnp.einsum(
        "thd,the->hde",
        as_float(keys) * weight.T[:, :, None],
        as_float(values),
        precision=HIGH_PRECISION,
    )


def backward_summary(queries, grads, labels, link, decay_rate):
    count = labels.shape[0]
    place = as_float(jnp.arange(count, dtype=jnp.int32))
    weight = jnp.where(
        (labels == labels[:1])[None, :] & link[None, :],
        jnp.exp(-decay_rate[:, None] * (place + 1.0)[None, :]),
        0.0,
    )
    return jnp.einsum(
        "thd,the->hde",
        as_float(queries) * weight.T[:, :, None],
        as_float(grads),
        precision=HIGH_PRECISION,
    )


def score_grads(probs, grads, value_part, delta):
    grad_probs = jnp.einsum("thd,uhd->htu", grads, value_part, preferred_element_type=jnp.float32)
    return (probs * (grad_probs - delta.T[:, :, None])).astype(jnp.bfloat16)


def body(
    lin_query,
    lin_key,
    lin_value,
    decay_rate,
    norm_gain,
    lin_grad,
    soft_query,
    soft_key,
    soft_value,
    soft_grad,
    segments,
):
    tokens = lin_query.shape[0]
    heads = lin_query.shape[1] // HD
    scale = 1.0 / math.sqrt(HD)
    device = lax.axis_index("seq")
    blocks_each = tokens // BLK
    pad_blocks = REACH * blocks_each
    padded = jnp.concatenate(
        [jnp.full((pad_blocks,), -1, jnp.int32), segments, jnp.full((pad_blocks,), -2, jnp.int32)]
    )
    window_blocks = lax.dynamic_slice_in_dim(
        padded, device * blocks_each, (2 * REACH + 1) * blocks_each
    )
    window_labels = jnp.broadcast_to(window_blocks[:, None], (window_blocks.shape[0], BLK)).reshape(-1)
    own_labels = window_labels[REACH * tokens : (REACH + 1) * tokens]
    key_labels = window_labels[tokens : (REACH + 1) * tokens]

    def split_heads(array):
        return array.reshape(tokens, heads, HD)

    queries = split_heads(lin_query)
    keys = split_heads(lin_key)
    values = split_heads(lin_value)
    soft_queries = split_heads(soft_query)
    soft_keys = split_heads(soft_key)
    soft_values = split_heads(soft_value)
    soft_grads = split_heads(soft_grad)
    span = 2 * REACH + 1
    firsts = window_blocks[::blocks_each]
    lasts = window_blocks[blocks_each - 1 :: blocks_each]
    summary = forward_summary(
        keys, values, own_labels, lasts[REACH : REACH + 1] == firsts[REACH + 1 : REACH + 2], decay_rate
    )
    full_decay = jnp.exp(-decay_rate * tokens)
    ahead = jnp.where((firsts[:-1] == firsts[1:])[:, None], full_decay[None, :], 0.0)
    behind = jnp.where(
        ((firsts[1:] == lasts[:-1]) & (firsts[1:] == lasts[1:]))[:, None], full_decay[None, :], 0.0
    )
    kv_shape = soft_keys.shape
    state_shape = summary.shape
    unit = packed(soft_keys, soft_values, summary.astype(jnp.bfloat16))
    size = unit.shape[0]
    two_back = shifted(unit, "seq", 2)
    four_back = shifted(two_back, "seq", 2)
    odd_back = shifted(jnp.concatenate([unit, two_back]), "seq", 1)
    five_back = shifted(four_back, "seq", 1)
    arrived = {
        1: odd_back[:size],
        2: two_back,
        3: odd_back[size:],
        4: four_back,
        5: five_back,
    }
    received = []
    state_in = jnp.zeros_like(summary)
    for back in range(1, REACH):
        got_key, got_value, got_state = unpacked(arrived[back], (kv_shape, kv_shape, state_shape))
        received.append((got_key, got_value))
        chain = jnp.prod(ahead[REACH - back + 1 : REACH], axis=0)
        state_in = state_in + chain[:, None, None] * as_float(got_state)
    decay = decay_matrix(own_labels, decay_rate)
    scores = jnp.einsum("thd,shd->hts", queries, keys, preferred_element_type=jnp.float32)
    weights = (decay * scores).astype(jnp.bfloat16)
    entry = entry_weights(own_labels, decay_rate)
    leave = exit_weights(own_labels, decay_rate)
    inner = jnp.einsum("hts,shd->thd", weights, values, preferred_element_type=jnp.float32)
    carried = jnp.einsum("thd,hde->the", as_float(queries), state_in, precision=HIGH_PRECISION)
    lin_out = inner + carried * entry.T[:, :, None]
    flat = lin_out.reshape(tokens, heads * HD)
    scaled_grad = norm_gain[None, :] * as_float(lin_grad)
    key_window = jnp.concatenate(
        [received[back - 1][0] for back in range(REACH - 1, 0, -1)] + [soft_keys], 0
    )
    value_window = jnp.concatenate(
        [received[back - 1][1] for back in range(REACH - 1, 0, -1)] + [soft_values], 0
    )
    query_place = jnp.arange(tokens, dtype=jnp.int32)
    key_place = jnp.arange(REACH * tokens, dtype=jnp.int32) - (REACH - 1) * tokens
    visible = (key_labels[None, :] == own_labels[:, None]) & (
        key_place[None, :] <= query_place[:, None]
    )
    soft_scores = (
        jnp.einsum("thd,uhd->htu", soft_queries, key_window, preferred_element_type=jnp.float32)
        * scale
    )
    soft_scores = jnp.where(visible[None], soft_scores, -jnp.inf)
    top = jnp.max(soft_scores, axis=-1)
    expo = jnp.exp(soft_scores - top[..., None])
    total = jnp.sum(expo, axis=-1)
    probs = expo / total[..., None]
    probs_half = probs.astype(jnp.bfloat16)
    attended = jnp.einsum(
        "htu,uhd->thd", probs_half, value_window, preferred_element_type=jnp.float32
    )
    delta = jnp.sum(as_float(soft_grads) * attended, axis=-1)
    grad_scores = score_grads(probs, soft_grads, value_window, delta)
    soft_query_grad = (
        jnp.einsum("htu,uhd->thd", grad_scores, key_window, preferred_element_type=jnp.float32)
        * scale
    )
    key_terms = (
        jnp.einsum("htu,thd->uhd", grad_scores, soft_queries, preferred_element_type=jnp.float32)
        * scale
    )
    value_terms = jnp.einsum(
        "htu,thd->uhd", probs_half, soft_grads, preferred_element_type=jnp.float32
    )
    soft_items = [
        packed(
            key_terms[(REACH - 1 - back) * tokens : (REACH - back) * tokens],
            value_terms[(REACH - 1 - back) * tokens : (REACH - back) * tokens],
        ).astype(jnp.bfloat16)
        for back in range(1, REACH)
    ]
    row_sums = jnp.stack([jnp.sum(flat * flat, axis=1), jnp.sum(flat * scaled_grad, axis=1)])
    row_sums, soft_items = lax.optimization_barrier((row_sums, soft_items))
    soft_arrived = [
        shifted(item, "seq", -back) for back, item in zip(range(1, REACH), soft_items)
    ]
    sums = tp_sum(row_sums, "tp")
    width = lax.axis_size("tp") * heads * HD
    inverse = lax.rsqrt(sums[0] / width + NORM_EPS)
    cross = sums[1] / width
    norm_grad = (inverse[:, None] * scaled_grad - flat * (inverse**3 * cross)[:, None]).astype(
        jnp.bfloat16
    )
    grad_heads = split_heads(norm_grad)
    back_summary = backward_summary(
        queries, grad_heads, own_labels, firsts[REACH : REACH + 1] == lasts[REACH - 1 : REACH], decay_rate
    )
    back_state = back_summary.astype(jnp.bfloat16)
    grad_scores_lin = jnp.einsum(
        "thd,shd->hts", grad_heads, values, preferred_element_type=jnp.float32
    )
    grad_weights = (decay * grad_scores_lin).astype(jnp.bfloat16)
    lin_query_grad = jnp.einsum(
        "hts,shd->thd", grad_weights, keys, preferred_element_type=jnp.float32
    )
    lin_query_grad = (
        lin_query_grad
        + jnp.einsum("the,hde->thd", as_float(grad_heads), state_in, precision=HIGH_PRECISION)
        * entry.T[:, :, None]
    )
    lin_key_grad = jnp.einsum(
        "hts,thd->shd", grad_weights, queries, preferred_element_type=jnp.float32
    )

    lin_value_grad = jnp.einsum(
        "hts,the->she", weights, grad_heads, preferred_element_type=jnp.float32
    )

    soft_key_grad = key_terms[(REACH - 1) * tokens :]
    soft_value_grad = value_terms[(REACH - 1) * tokens :]
    items = {}
    for back in range(1, REACH):
        chain = jnp.prod(behind[REACH - back : REACH - 1], axis=0)
        items[back] = (chain[:, None, None] * back_summary).reshape(-1)
    size = items[1].shape[0]

    def wire(value):
        return value.astype(jnp.bfloat16)

    first = as_float(shifted(wire(jnp.concatenate([items[5], items[3], items[1]])), "seq", -1))
    second = as_float(
        shifted(
            wire(jnp.concatenate([items[2] + first[size : 2 * size], items[4] + first[:size]])),
            "seq",
            -2,
        )
    )
    third = as_float(shifted(wire(second[size:]), "seq", -2))
    reverse_in = (first[2 * size :] + second[:size] + third).reshape(state_shape)
    for got in soft_arrived:
        got_key, got_value = unpacked(as_float(got), (kv_shape, kv_shape))
        soft_key_grad = soft_key_grad + got_key
        soft_value_grad = soft_value_grad + got_value
    lin_key_grad = lin_key_grad + (
        jnp.einsum("she,hde->shd", as_float(values), reverse_in, precision=HIGH_PRECISION)
        * leave.T[:, :, None]
    )
    lin_value_grad = lin_value_grad + (
        jnp.einsum("shd,hde->she", as_float(keys), reverse_in, precision=HIGH_PRECISION)
        * leave.T[:, :, None]
    )

    def merge_heads(array):
        return array.reshape(tokens, heads * HD).astype(jnp.bfloat16)

    return (
        merge_heads(lin_query_grad),
        merge_heads(lin_key_grad),
        merge_heads(lin_value_grad),
        merge_heads(soft_query_grad),
        merge_heads(soft_key_grad),
        merge_heads(soft_value_grad),
    )


def solution(mesh):
    return jax.shard_map(
        body,
        mesh=mesh,
        in_specs=(
            P("seq", "tp"),
            P("seq", "tp"),
            P("seq", "tp"),
            P("tp"),
            P("tp"),
            P("seq", "tp"),
            P("seq", "tp"),
            P("seq", "tp"),
            P("seq", "tp"),
            P("seq", "tp"),
            P(),
        ),
        out_specs=(
            P("seq", "tp"),
            P("seq", "tp"),
            P("seq", "tp"),
            P("seq", "tp"),
            P("seq", "tp"),
            P("seq", "tp"),
        ),
        check_vma=False,
    )
```

```python
import math

import jax
import jax.numpy as jnp
from jax import lax
from jax.sharding import PartitionSpec as P

HD = 128
BLK = 128
REACH = 6


HIGH_PRECISION = lax.Precision.HIGHEST
NORM_EPS = 1e-06


def shifted(value, axis, steps):
    count = lax.axis_size(axis)
    first, last = (max(0, -steps), min(count, count - steps))
    return lax.ppermute(value, axis, [(source, source + steps) for source in range(first, last)])


def tp_sum(value, axis):
    return jnp.sum(lax.all_gather(value, axis), axis=0)


def packed(*parts):
    return jnp.concatenate([part.reshape(-1) for part in parts])


def unpacked(flat, shapes):
    out, at = [], 0
    for shape in shapes:
        size = math.prod(shape)
        out.append(flat[at : at + size].reshape(shape))
        at += size
    return out


def as_float(array):
    return array.astype(jnp.float32)


def decay_matrix(labels, decay_rate):
    place = jnp.arange(labels.shape[0], dtype=jnp.int32)
    distance = as_float(place[:, None] - place[None, :])
    visible = (labels[:, None] == labels[None, :]) & (distance >= 0)
    return jnp.where(
        visible[None], jnp.exp(-decay_rate[:, None, None] * jnp.maximum(distance, 0.0)[None]), 0.0
    )


def entry_weights(labels, decay_rate):
    place = as_float(jnp.arange(labels.shape[0], dtype=jnp.int32))
    return jnp.where(
        (labels == labels[:1])[None, :], jnp.exp(-decay_rate[:, None] * place[None, :]), 0.0
    )


def exit_weights(labels, decay_rate):
    count = labels.shape[0]
    place = as_float(jnp.arange(count, dtype=jnp.int32))
    return jnp.where(
        (labels == labels[-1:])[None, :],
        jnp.exp(-decay_rate[:, None] * (count - 1 - place)[None, :]),
        0.0,
    )


def forward_summary(keys, values, labels, link, decay_rate):
    count = labels.shape[0]
    place = as_float(jnp.arange(count, dtype=jnp.int32))
    weight = jnp.where(
        (labels == labels[-1:])[None, :] & link[None, :],
        jnp.exp(-decay_rate[:, None] * (count - place)[None, :]),
        0.0,
    )
    return jnp.einsum(
        "thd,the->hde",
        as_float(keys) * weight.T[:, :, None],
        as_float(values),
        precision=HIGH_PRECISION,
    )


def backward_summary(queries, grads, labels, link, decay_rate):
    count = labels.shape[0]
    place = as_float(jnp.arange(count, dtype=jnp.int32))
    weight = jnp.where(
        (labels == labels[:1])[None, :] & link[None, :],
        jnp.exp(-decay_rate[:, None] * (place + 1.0)[None, :]),
        0.0,
    )
    return jnp.einsum(
        "thd,the->hde",
        as_float(queries) * weight.T[:, :, None],
        as_float(grads),
        precision=HIGH_PRECISION,
    )


def score_grads(probs, grads, value_part, delta):
    grad_probs = jnp.einsum("thd,uhd->htu", grads, value_part, preferred_element_type=jnp.float32)
    return (probs * (grad_probs - delta.T[:, :, None])).astype(jnp.bfloat16)


def body(
    lin_query,
    lin_key,
    lin_value,
    decay_rate,
    norm_gain,
    lin_grad,
    soft_query,
    soft_key,
    soft_value,
    soft_grad,
    segments,
):
    tokens = lin_query.shape[0]
    heads = lin_query.shape[1] // HD
    scale = 1.0 / math.sqrt(HD)
    device = lax.axis_index("seq")
    blocks_each = tokens // BLK
    pad_blocks = REACH * blocks_each
    padded = jnp.concatenate(
        [jnp.full((pad_blocks,), -1, jnp.int32), segments, jnp.full((pad_blocks,), -2, jnp.int32)]
    )
    window_blocks = lax.dynamic_slice_in_dim(
        padded, device * blocks_each, (2 * REACH + 1) * blocks_each
    )
    window_labels = jnp.broadcast_to(window_blocks[:, None], (window_blocks.shape[0], BLK)).reshape(-1)
    own_labels = window_labels[REACH * tokens : (REACH + 1) * tokens]
    key_labels = window_labels[tokens : (REACH + 1) * tokens]

    def split_heads(array):
        return array.reshape(tokens, heads, HD)

    queries = split_heads(lin_query)
    keys = split_heads(lin_key)
    values = split_heads(lin_value)
    soft_queries = split_heads(soft_query)
    soft_keys = split_heads(soft_key)
    soft_values = split_heads(soft_value)
    soft_grads = split_heads(soft_grad)
    span = 2 * REACH + 1
    firsts = window_blocks[::blocks_each]
    lasts = window_blocks[blocks_each - 1 :: blocks_each]
    summary = forward_summary(
        keys, values, own_labels, lasts[REACH : REACH + 1] == firsts[REACH + 1 : REACH + 2], decay_rate
    )
    full_decay = jnp.exp(-decay_rate * tokens)
    ahead = jnp.where((firsts[:-1] == firsts[1:])[:, None], full_decay[None, :], 0.0)
    behind = jnp.where(
        ((firsts[1:] == lasts[:-1]) & (firsts[1:] == lasts[1:]))[:, None], full_decay[None, :], 0.0
    )
    kv_shape = soft_keys.shape
    state_shape = summary.shape
    unit = packed(soft_keys, soft_values, summary.astype(jnp.bfloat16))
    size = unit.shape[0]
    two_back = shifted(unit, "seq", 2)
    four_back = shifted(two_back, "seq", 2)
    odd_back = shifted(jnp.concatenate([unit, two_back]), "seq", 1)
    five_back = shifted(four_back, "seq", 1)
    arrived = {
        1: odd_back[:size],
        2: two_back,
        3: odd_back[size:],
        4: four_back,
        5: five_back,
    }
    received = []
    state_in = jnp.zeros_like(summary)
    for back in range(1, REACH):
        got_key, got_value, got_state = unpacked(arrived[back], (kv_shape, kv_shape, state_shape))
        received.append((got_key, got_value))
        chain = jnp.prod(ahead[REACH - back + 1 : REACH], axis=0)
        state_in = state_in + chain[:, None, None] * as_float(got_state)
    decay = decay_matrix(own_labels, decay_rate)
    scores = jnp.einsum("thd,shd->hts", queries, keys, preferred_element_type=jnp.float32)
    weights = (decay * scores).astype(jnp.bfloat16)
    entry = entry_weights(own_labels, decay_rate)
    leave = exit_weights(own_labels, decay_rate)
    inner = jnp.einsum("hts,shd->thd", weights, values, preferred_element_type=jnp.float32)
    carried = jnp.einsum("thd,hde->the", as_float(queries), state_in, precision=HIGH_PRECISION)
    lin_out = inner + carried * entry.T[:, :, None]
    flat = lin_out.reshape(tokens, heads * HD)
    scaled_grad = norm_gain[None, :] * as_float(lin_grad)
    pieces = flat.reshape(tokens, 64, -1)
    grad_pieces = scaled_grad.reshape(tokens, 64, -1)
    sums = tp_sum(jnp.stack([jnp.sum(pieces * pieces, axis=2), jnp.sum(pieces * grad_pieces, axis=2)]).transpose(2, 0, 1), "tp")
    sums = jnp.sum(sums, axis=0)
    width = lax.axis_size("tp") * heads * HD
    inverse = lax.rsqrt(sums[0] / width + NORM_EPS)
    cross = sums[1] / width
    norm_grad = (inverse[:, None] * scaled_grad - flat * (inverse**3 * cross)[:, None]).astype(
        jnp.bfloat16
    )
    grad_heads = split_heads(norm_grad)
    back_summary = backward_summary(
        queries, grad_heads, own_labels, firsts[REACH : REACH + 1] == lasts[REACH - 1 : REACH], decay_rate
    )
    back_state = back_summary.astype(jnp.bfloat16)
    grad_scores_lin = jnp.einsum(
        "thd,shd->hts", grad_heads, values, preferred_element_type=jnp.float32
    )
    grad_weights = (decay * grad_scores_lin).astype(jnp.bfloat16)
    lin_query_grad = jnp.einsum(
        "hts,shd->thd", grad_weights, keys, preferred_element_type=jnp.float32
    )
    lin_query_grad = (
        lin_query_grad
        + jnp.einsum("the,hde->thd", as_float(grad_heads), state_in, precision=HIGH_PRECISION)
        * entry.T[:, :, None]
    )
    lin_key_grad = jnp.einsum(
        "hts,thd->shd", grad_weights, queries, preferred_element_type=jnp.float32
    )

    lin_value_grad = jnp.einsum(
        "hts,the->she", weights, grad_heads, preferred_element_type=jnp.float32
    )

    key_window = jnp.concatenate(
        [received[back - 1][0] for back in range(REACH - 1, 0, -1)] + [soft_keys], 0
    )
    value_window = jnp.concatenate(
        [received[back - 1][1] for back in range(REACH - 1, 0, -1)] + [soft_values], 0
    )
    query_place = jnp.arange(tokens, dtype=jnp.int32)
    key_place = jnp.arange(REACH * tokens, dtype=jnp.int32) - (REACH - 1) * tokens
    visible = (key_labels[None, :] == own_labels[:, None]) & (
        key_place[None, :] <= query_place[:, None]
    )
    soft_scores = (
        jnp.einsum("thd,uhd->htu", soft_queries, key_window, preferred_element_type=jnp.float32)
        * scale
    )
    soft_scores = jnp.where(visible[None], soft_scores, -jnp.inf)
    top = jnp.max(soft_scores, axis=-1)
    expo = jnp.exp(soft_scores - top[..., None])
    total = jnp.sum(expo, axis=-1)
    probs = expo / total[..., None]
    probs_half = probs.astype(jnp.bfloat16)
    attended = jnp.einsum(
        "htu,uhd->thd", probs_half, value_window, preferred_element_type=jnp.float32
    )
    delta = jnp.sum(as_float(soft_grads) * attended, axis=-1)
    grad_scores = score_grads(probs, soft_grads, value_window, delta)
    soft_query_grad = (
        jnp.einsum("htu,uhd->thd", grad_scores, key_window, preferred_element_type=jnp.float32)
        * scale
    )
    key_terms = (
        jnp.einsum("htu,thd->uhd", grad_scores, soft_queries, preferred_element_type=jnp.float32)
        * scale
    )
    value_terms = jnp.einsum(
        "htu,thd->uhd", probs_half, soft_grads, preferred_element_type=jnp.float32
    )
    soft_key_grad = key_terms[(REACH - 1) * tokens :]
    soft_value_grad = value_terms[(REACH - 1) * tokens :]
    items = {}
    for back in range(1, REACH):
        lower = (REACH - 1 - back) * tokens
        chain = jnp.prod(behind[REACH - back : REACH - 1], axis=0)
        items[back] = packed(
            key_terms[lower : lower + tokens],
            value_terms[lower : lower + tokens],
            chain[:, None, None] * back_summary,
        )
    size = items[1].shape[0]

    def wire(value):
        return value.astype(jnp.bfloat16)

    first = as_float(shifted(wire(jnp.concatenate([items[5], items[3], items[1]])), "seq", -1))
    second = as_float(
        shifted(
            wire(jnp.concatenate([items[2] + first[size : 2 * size], items[4] + first[:size]])),
            "seq",
            -2,
        )
    )
    third = as_float(shifted(wire(second[size:]), "seq", -2))
    total = first[2 * size :] + second[:size] + third
    got_key, got_value, reverse_in = unpacked(total, (kv_shape, kv_shape, state_shape))
    soft_key_grad = soft_key_grad + got_key
    soft_value_grad = soft_value_grad + got_value
    lin_key_grad = lin_key_grad + (
        jnp.einsum("she,hde->shd", as_float(values), reverse_in, precision=HIGH_PRECISION)
        * leave.T[:, :, None]
    )
    lin_value_grad = lin_value_grad + (
        jnp.einsum("shd,hde->she", as_float(keys), reverse_in, precision=HIGH_PRECISION)
        * leave.T[:, :, None]
    )

    def merge_heads(array):
        return array.reshape(tokens, heads * HD).astype(jnp.bfloat16)

    return (
        merge_heads(lin_query_grad),
        merge_heads(lin_key_grad),
        merge_heads(lin_value_grad),
        merge_heads(soft_query_grad),
        merge_heads(soft_key_grad),
        merge_heads(soft_value_grad),
    )


def solution(mesh):
    return jax.shard_map(
        body,
        mesh=mesh,
        in_specs=(
            P("seq", "tp"),
            P("seq", "tp"),
            P("seq", "tp"),
            P("tp"),
            P("tp"),
            P("seq", "tp"),
            P("seq", "tp"),
            P("seq", "tp"),
            P("seq", "tp"),
            P("seq", "tp"),
            P(),
        ),
        out_specs=(
            P("seq", "tp"),
            P("seq", "tp"),
            P("seq", "tp"),
            P("seq", "tp"),
            P("seq", "tp"),
            P("seq", "tp"),
        ),
        check_vma=False,
    )
```

```python
import math

import jax
import jax.numpy as jnp
from jax import lax
from jax.sharding import PartitionSpec as P

HD = 128
BLK = 128
REACH = 6


HIGH_PRECISION = lax.Precision.HIGHEST
NORM_EPS = 1e-06
TP = ("tp_outer", "tp_inner")


def shifted(value, axis, steps):
    count = lax.axis_size(axis)
    first, last = (max(0, -steps), min(count, count - steps))
    return lax.ppermute(value, axis, [(source, source + steps) for source in range(first, last)])


def tp_sum(value, axes):
    for axis in reversed(axes):
        value = jnp.sum(lax.all_gather(value, axis), axis=0)
    return value


def packed(*parts):
    return jnp.concatenate([part.reshape(-1) for part in parts])


def unpacked(flat, shapes):
    out, at = [], 0
    for shape in shapes:
        size = math.prod(shape)
        out.append(flat[at : at + size].reshape(shape))
        at += size
    return out


def as_float(array):
    return array.astype(jnp.float32)


def decay_matrix(labels, decay_rate):
    place = jnp.arange(labels.shape[0], dtype=jnp.int32)
    distance = as_float(place[:, None] - place[None, :])
    visible = (labels[:, None] == labels[None, :]) & (distance >= 0)
    return jnp.where(
        visible[None], jnp.exp(-decay_rate[:, None, None] * jnp.maximum(distance, 0.0)[None]), 0.0
    )


def entry_weights(labels, decay_rate):
    place = as_float(jnp.arange(labels.shape[0], dtype=jnp.int32))
    return jnp.where(
        (labels == labels[:1])[None, :], jnp.exp(-decay_rate[:, None] * place[None, :]), 0.0
    )


def exit_weights(labels, decay_rate):
    count = labels.shape[0]
    place = as_float(jnp.arange(count, dtype=jnp.int32))
    return jnp.where(
        (labels == labels[-1:])[None, :],
        jnp.exp(-decay_rate[:, None] * (count - 1 - place)[None, :]),
        0.0,
    )


def forward_summary(keys, values, labels, link, decay_rate):
    count = labels.shape[0]
    place = as_float(jnp.arange(count, dtype=jnp.int32))
    weight = jnp.where(
        (labels == labels[-1:])[None, :] & link[None, :],
        jnp.exp(-decay_rate[:, None] * (count - place)[None, :]),
        0.0,
    )
    return jnp.einsum(
        "thd,the->hde",
        as_float(keys) * weight.T[:, :, None],
        as_float(values),
        precision=HIGH_PRECISION,
    )


def backward_summary(queries, grads, labels, link, decay_rate):
    count = labels.shape[0]
    place = as_float(jnp.arange(count, dtype=jnp.int32))
    weight = jnp.where(
        (labels == labels[:1])[None, :] & link[None, :],
        jnp.exp(-decay_rate[:, None] * (place + 1.0)[None, :]),
        0.0,
    )
    return jnp.einsum(
        "thd,the->hde",
        as_float(queries) * weight.T[:, :, None],
        as_float(grads),
        precision=HIGH_PRECISION,
    )


def score_grads(probs, grads, value_part, delta):
    grad_probs = jnp.einsum("thd,uhd->htu", grads, value_part, preferred_element_type=jnp.float32)
    return (probs * (grad_probs - delta.T[:, :, None])).astype(jnp.bfloat16)


def body(
    lin_query,
    lin_key,
    lin_value,
    decay_rate,
    norm_gain,
    lin_grad,
    soft_query,
    soft_key,
    soft_value,
    soft_grad,
    segments,
):
    tokens = lin_query.shape[0]
    heads = lin_query.shape[1] // HD
    scale = 1.0 / math.sqrt(HD)
    device = lax.axis_index("seq")
    blocks_each = tokens // BLK
    pad_blocks = REACH * blocks_each
    padded = jnp.concatenate(
        [jnp.full((pad_blocks,), -1, jnp.int32), segments, jnp.full((pad_blocks,), -2, jnp.int32)]
    )
    window_blocks = lax.dynamic_slice_in_dim(
        padded, device * blocks_each, (2 * REACH + 1) * blocks_each
    )
    window_labels = jnp.broadcast_to(window_blocks[:, None], (window_blocks.shape[0], BLK)).reshape(-1)
    own_labels = window_labels[REACH * tokens : (REACH + 1) * tokens]
    key_labels = window_labels[tokens : (REACH + 1) * tokens]

    def split_heads(array):
        return array.reshape(tokens, heads, HD)

    queries = split_heads(lin_query)
    keys = split_heads(lin_key)
    values = split_heads(lin_value)
    soft_queries = split_heads(soft_query)
    soft_keys = split_heads(soft_key)
    soft_values = split_heads(soft_value)
    soft_grads = split_heads(soft_grad)
    span = 2 * REACH + 1
    firsts = window_blocks[::blocks_each]
    lasts = window_blocks[blocks_each - 1 :: blocks_each]
    summary = forward_summary(
        keys, values, own_labels, lasts[REACH : REACH + 1] == firsts[REACH + 1 : REACH + 2], decay_rate
    )
    full_decay = jnp.exp(-decay_rate * tokens)
    ahead = jnp.where((firsts[:-1] == firsts[1:])[:, None], full_decay[None, :], 0.0)
    behind = jnp.where(
        ((firsts[1:] == lasts[:-1]) & (firsts[1:] == lasts[1:]))[:, None], full_decay[None, :], 0.0
    )
    kv_shape = soft_keys.shape
    state_shape = summary.shape
    unit = packed(soft_keys, soft_values, summary.astype(jnp.bfloat16))
    size = unit.shape[0]
    two_back = shifted(unit, "seq", 2)
    four_back = shifted(two_back, "seq", 2)
    odd_back = shifted(jnp.concatenate([unit, two_back]), "seq", 1)
    five_back = shifted(four_back, "seq", 1)
    arrived = {
        1: odd_back[:size],
        2: two_back,
        3: odd_back[size:],
        4: four_back,
        5: five_back,
    }
    received = []
    state_in = jnp.zeros_like(summary)
    for back in range(1, REACH):
        got_key, got_value, got_state = unpacked(arrived[back], (kv_shape, kv_shape, state_shape))
        received.append((got_key, got_value))
        chain = jnp.prod(ahead[REACH - back + 1 : REACH], axis=0)
        state_in = state_in + chain[:, None, None] * as_float(got_state)
    decay = decay_matrix(own_labels, decay_rate)
    scores = jnp.einsum("thd,shd->hts", queries, keys, preferred_element_type=jnp.float32)
    weights = (decay * scores).astype(jnp.bfloat16)
    entry = entry_weights(own_labels, decay_rate)
    leave = exit_weights(own_labels, decay_rate)
    inner = jnp.einsum("hts,shd->thd", weights, values, preferred_element_type=jnp.float32)
    carried = jnp.einsum("thd,hde->the", as_float(queries), state_in, precision=HIGH_PRECISION)
    lin_out = inner + carried * entry.T[:, :, None]
    flat = lin_out.reshape(tokens, heads * HD)
    scaled_grad = norm_gain[None, :] * as_float(lin_grad)
    sums = tp_sum(jnp.stack([jnp.sum(flat * flat, axis=1), jnp.sum(flat * scaled_grad, axis=1)]), TP)
    width = lax.axis_size(TP) * heads * HD
    inverse = lax.rsqrt(sums[0] / width + NORM_EPS)
    cross = sums[1] / width
    norm_grad = (inverse[:, None] * scaled_grad - flat * (inverse**3 * cross)[:, None]).astype(
        jnp.bfloat16
    )
    grad_heads = split_heads(norm_grad)
    back_summary = backward_summary(
        queries, grad_heads, own_labels, firsts[REACH : REACH + 1] == lasts[REACH - 1 : REACH], decay_rate
    )
    back_state = back_summary.astype(jnp.bfloat16)
    grad_scores_lin = jnp.einsum(
        "thd,shd->hts", grad_heads, values, preferred_element_type=jnp.float32
    )
    grad_weights = (decay * grad_scores_lin).astype(jnp.bfloat16)
    lin_query_grad = jnp.einsum(
        "hts,shd->thd", grad_weights, keys, preferred_element_type=jnp.float32
    )
    lin_query_grad = (
        lin_query_grad
        + jnp.einsum("the,hde->thd", as_float(grad_heads), state_in, precision=HIGH_PRECISION)
        * entry.T[:, :, None]
    )
    lin_key_grad = jnp.einsum(
        "hts,thd->shd", grad_weights, queries, preferred_element_type=jnp.float32
    )

    lin_value_grad = jnp.einsum(
        "hts,the->she", weights, grad_heads, preferred_element_type=jnp.float32
    )

    key_window = jnp.concatenate(
        [received[back - 1][0] for back in range(REACH - 1, 0, -1)] + [soft_keys], 0
    )
    value_window = jnp.concatenate(
        [received[back - 1][1] for back in range(REACH - 1, 0, -1)] + [soft_values], 0
    )
    query_place = jnp.arange(tokens, dtype=jnp.int32)
    key_place = jnp.arange(REACH * tokens, dtype=jnp.int32) - (REACH - 1) * tokens
    visible = (key_labels[None, :] == own_labels[:, None]) & (
        key_place[None, :] <= query_place[:, None]
    )
    soft_scores = (
        jnp.einsum("thd,uhd->htu", soft_queries, key_window, preferred_element_type=jnp.float32)
        * scale
    )
    soft_scores = jnp.where(visible[None], soft_scores, -jnp.inf)
    top = jnp.max(soft_scores, axis=-1)
    expo = jnp.exp(soft_scores - top[..., None])
    total = jnp.sum(expo, axis=-1)
    probs = expo / total[..., None]
    probs_half = probs.astype(jnp.bfloat16)
    attended = jnp.einsum(
        "htu,uhd->thd", probs_half, value_window, preferred_element_type=jnp.float32
    )
    delta = jnp.sum(as_float(soft_grads) * attended, axis=-1)
    grad_scores = score_grads(probs, soft_grads, value_window, delta)
    soft_query_grad = (
        jnp.einsum("htu,uhd->thd", grad_scores, key_window, preferred_element_type=jnp.float32)
        * scale
    )
    key_terms = (
        jnp.einsum("htu,thd->uhd", grad_scores, soft_queries, preferred_element_type=jnp.float32)
        * scale
    )
    value_terms = jnp.einsum(
        "htu,thd->uhd", probs_half, soft_grads, preferred_element_type=jnp.float32
    )
    soft_key_grad = key_terms[(REACH - 1) * tokens :]
    soft_value_grad = value_terms[(REACH - 1) * tokens :]
    items = {}
    for back in range(1, REACH):
        lower = (REACH - 1 - back) * tokens
        chain = jnp.prod(behind[REACH - back : REACH - 1], axis=0)
        items[back] = packed(
            key_terms[lower : lower + tokens],
            value_terms[lower : lower + tokens],
            chain[:, None, None] * back_summary,
        )
    size = items[1].shape[0]

    def wire(value):
        return value.astype(jnp.bfloat16)

    first = as_float(shifted(wire(jnp.concatenate([items[5], items[3], items[1]])), "seq", -1))
    second = as_float(
        shifted(
            wire(jnp.concatenate([items[2] + first[size : 2 * size], items[4] + first[:size]])),
            "seq",
            -2,
        )
    )
    third = as_float(shifted(wire(second[size:]), "seq", -2))
    total = first[2 * size :] + second[:size] + third
    got_key, got_value, reverse_in = unpacked(total, (kv_shape, kv_shape, state_shape))
    soft_key_grad = soft_key_grad + got_key
    soft_value_grad = soft_value_grad + got_value
    lin_key_grad = lin_key_grad + (
        jnp.einsum("she,hde->shd", as_float(values), reverse_in, precision=HIGH_PRECISION)
        * leave.T[:, :, None]
    )
    lin_value_grad = lin_value_grad + (
        jnp.einsum("shd,hde->she", as_float(keys), reverse_in, precision=HIGH_PRECISION)
        * leave.T[:, :, None]
    )

    def merge_heads(array):
        return array.reshape(tokens, heads * HD).astype(jnp.bfloat16)

    return (
        merge_heads(lin_query_grad),
        merge_heads(lin_key_grad),
        merge_heads(lin_value_grad),
        merge_heads(soft_query_grad),
        merge_heads(soft_key_grad),
        merge_heads(soft_value_grad),
    )


def split_mesh(mesh):
    count = mesh.shape["tp"]
    inner = math.isqrt(count)
    if inner * inner != count:
        inner = 1
    devices = mesh.devices.reshape(mesh.shape["seq"], count // inner, inner)
    return jax.sharding.Mesh(devices, ("seq",) + TP)


def solution(mesh):
    return jax.shard_map(
        body,
        mesh=split_mesh(mesh),
        in_specs=(
            P("seq", TP),
            P("seq", TP),
            P("seq", TP),
            P(TP),
            P(TP),
            P("seq", TP),
            P("seq", TP),
            P("seq", TP),
            P("seq", TP),
            P("seq", TP),
            P(),
        ),
        out_specs=(
            P("seq", TP),
            P("seq", TP),
            P("seq", TP),
            P("seq", TP),
            P("seq", TP),
            P("seq", TP),
        ),
        check_vma=False,
    )
```

```python
import math

import jax
import jax.numpy as jnp
from jax import lax
from jax.sharding import PartitionSpec as P

HD = 128
BLK = 128
REACH = 6


HIGH_PRECISION = lax.Precision.HIGHEST
NORM_EPS = 1e-06
TP = ("tp_outer", "tp_inner")


def shifted(value, axis, steps):
    count = lax.axis_size(axis)
    first, last = (max(0, -steps), min(count, count - steps))
    return lax.ppermute(value, axis, [(source, source + steps) for source in range(first, last)])


def tp_sum(value, axes):
    for axis in reversed(axes):
        value = jnp.sum(lax.all_gather(value, axis), axis=0)
    return value


def packed(*parts):
    return jnp.concatenate([part.reshape(-1, part.shape[-1]) for part in parts], 0)


def unpacked(block, shapes):
    out, at = [], 0
    for shape in shapes:
        rows = math.prod(shape) // block.shape[1]
        out.append(block[at : at + rows].reshape(shape))
        at += rows
    return out


def as_float(array):
    return array.astype(jnp.float32)


def decay_matrix(labels, decay_rate):
    place = jnp.arange(labels.shape[0], dtype=jnp.int32)
    distance = as_float(place[:, None] - place[None, :])
    visible = (labels[:, None] == labels[None, :]) & (distance >= 0)
    return jnp.where(
        visible[None], jnp.exp(-decay_rate[:, None, None] * jnp.maximum(distance, 0.0)[None]), 0.0
    )


def entry_weights(labels, decay_rate):
    place = as_float(jnp.arange(labels.shape[0], dtype=jnp.int32))
    return jnp.where(
        (labels == labels[:1])[None, :], jnp.exp(-decay_rate[:, None] * place[None, :]), 0.0
    )


def exit_weights(labels, decay_rate):
    count = labels.shape[0]
    place = as_float(jnp.arange(count, dtype=jnp.int32))
    return jnp.where(
        (labels == labels[-1:])[None, :],
        jnp.exp(-decay_rate[:, None] * (count - 1 - place)[None, :]),
        0.0,
    )


def forward_summary(keys, values, labels, link, decay_rate):
    count = labels.shape[0]
    place = as_float(jnp.arange(count, dtype=jnp.int32))
    weight = jnp.where(
        (labels == labels[-1:])[None, :] & link[None, :],
        jnp.exp(-decay_rate[:, None] * (count - place)[None, :]),
        0.0,
    )
    return jnp.einsum(
        "thd,the->hde",
        as_float(keys) * weight.T[:, :, None],
        as_float(values),
        precision=HIGH_PRECISION,
    )


def backward_summary(queries, grads, labels, link, decay_rate):
    count = labels.shape[0]
    place = as_float(jnp.arange(count, dtype=jnp.int32))
    weight = jnp.where(
        (labels == labels[:1])[None, :] & link[None, :],
        jnp.exp(-decay_rate[:, None] * (place + 1.0)[None, :]),
        0.0,
    )
    return jnp.einsum(
        "thd,the->hde",
        as_float(queries) * weight.T[:, :, None],
        as_float(grads),
        precision=HIGH_PRECISION,
    )


def score_grads(probs, grads, value_part, delta):
    grad_probs = jnp.einsum("thd,hud->htu", grads, value_part, preferred_element_type=jnp.float32)
    return (probs * (grad_probs - delta.T[:, :, None])).astype(jnp.bfloat16)


def body(
    lin_query,
    lin_key,
    lin_value,
    decay_rate,
    norm_gain,
    lin_grad,
    soft_query,
    soft_key,
    soft_value,
    soft_grad,
    segments,
):
    tokens = lin_query.shape[0]
    heads = lin_query.shape[1] // HD
    scale = 1.0 / math.sqrt(HD)
    device = lax.axis_index("seq")
    blocks_each = tokens // BLK
    pad_blocks = REACH * blocks_each
    padded = jnp.concatenate(
        [jnp.full((pad_blocks,), -1, jnp.int32), segments, jnp.full((pad_blocks,), -2, jnp.int32)]
    )
    window_blocks = lax.dynamic_slice_in_dim(
        padded, device * blocks_each, (2 * REACH + 1) * blocks_each
    )
    window_labels = jnp.broadcast_to(window_blocks[:, None], (window_blocks.shape[0], BLK)).reshape(-1)
    own_labels = window_labels[REACH * tokens : (REACH + 1) * tokens]
    key_labels = window_labels[tokens : (REACH + 1) * tokens]

    def split_heads(array):
        return array.reshape(tokens, heads, HD)

    queries = split_heads(lin_query)
    keys = split_heads(lin_key)
    values = split_heads(lin_value)
    soft_queries = split_heads(soft_query)
    soft_keys = split_heads(soft_key)
    soft_values = split_heads(soft_value)
    soft_grads = split_heads(soft_grad)
    span = 2 * REACH + 1
    firsts = window_blocks[::blocks_each]
    lasts = window_blocks[blocks_each - 1 :: blocks_each]
    summary = forward_summary(
        keys, values, own_labels, lasts[REACH : REACH + 1] == firsts[REACH + 1 : REACH + 2], decay_rate
    )
    full_decay = jnp.exp(-decay_rate * tokens)
    ahead = jnp.where((firsts[:-1] == firsts[1:])[:, None], full_decay[None, :], 0.0)
    behind = jnp.where(
        ((firsts[1:] == lasts[:-1]) & (firsts[1:] == lasts[1:]))[:, None], full_decay[None, :], 0.0
    )
    key_major = soft_keys.transpose(1, 0, 2)
    value_major = soft_values.transpose(1, 0, 2)
    kv_shape = key_major.shape
    state_shape = summary.shape
    unit = packed(key_major, value_major, summary.astype(jnp.bfloat16))
    size = unit.shape[0]
    two_back = shifted(unit, "seq", 2)
    four_back = shifted(two_back, "seq", 2)
    odd_back = shifted(jnp.concatenate([unit, two_back]), "seq", 1)
    five_back = shifted(four_back, "seq", 1)
    arrived = {
        1: odd_back[:size],
        2: two_back,
        3: odd_back[size:],
        4: four_back,
        5: five_back,
    }
    received = []
    state_in = jnp.zeros_like(summary)
    for back in range(1, REACH):
        got_key, got_value, got_state = unpacked(arrived[back], (kv_shape, kv_shape, state_shape))
        received.append((got_key, got_value))
        chain = jnp.prod(ahead[REACH - back + 1 : REACH], axis=0)
        state_in = state_in + chain[:, None, None] * as_float(got_state)
    decay = decay_matrix(own_labels, decay_rate)
    scores = jnp.einsum("thd,shd->hts", queries, keys, preferred_element_type=jnp.float32)
    weights = (decay * scores).astype(jnp.bfloat16)
    entry = entry_weights(own_labels, decay_rate)
    leave = exit_weights(own_labels, decay_rate)
    inner = jnp.einsum("hts,shd->thd", weights, values, preferred_element_type=jnp.float32)
    carried = jnp.einsum("thd,hde->the", as_float(queries), state_in, precision=HIGH_PRECISION)
    lin_out = inner + carried * entry.T[:, :, None]
    flat = lin_out.reshape(tokens, heads * HD)
    scaled_grad = norm_gain[None, :] * as_float(lin_grad)
    sums = tp_sum(jnp.stack([jnp.sum(flat * flat, axis=1), jnp.sum(flat * scaled_grad, axis=1)]), TP)
    width = lax.axis_size(TP) * heads * HD
    inverse = lax.rsqrt(sums[0] / width + NORM_EPS)
    cross = sums[1] / width
    norm_grad = (inverse[:, None] * scaled_grad - flat * (inverse**3 * cross)[:, None]).astype(
        jnp.bfloat16
    )
    grad_heads = split_heads(norm_grad)
    back_summary = backward_summary(
        queries, grad_heads, own_labels, firsts[REACH : REACH + 1] == lasts[REACH - 1 : REACH], decay_rate
    )
    back_state = back_summary.astype(jnp.bfloat16)
    grad_scores_lin = jnp.einsum(
        "thd,shd->hts", grad_heads, values, preferred_element_type=jnp.float32
    )
    grad_weights = (decay * grad_scores_lin).astype(jnp.bfloat16)
    lin_query_grad = jnp.einsum(
        "hts,shd->thd", grad_weights, keys, preferred_element_type=jnp.float32
    )
    lin_query_grad = (
        lin_query_grad
        + jnp.einsum("the,hde->thd", as_float(grad_heads), state_in, precision=HIGH_PRECISION)
        * entry.T[:, :, None]
    )
    lin_key_grad = jnp.einsum(
        "hts,thd->shd", grad_weights, queries, preferred_element_type=jnp.float32
    )

    lin_value_grad = jnp.einsum(
        "hts,the->she", weights, grad_heads, preferred_element_type=jnp.float32
    )

    key_window = jnp.concatenate(
        [received[back - 1][0] for back in range(REACH - 1, 0, -1)] + [key_major], 1
    )
    value_window = jnp.concatenate(
        [received[back - 1][1] for back in range(REACH - 1, 0, -1)] + [value_major], 1
    )
    query_place = jnp.arange(tokens, dtype=jnp.int32)
    key_place = jnp.arange(REACH * tokens, dtype=jnp.int32) - (REACH - 1) * tokens
    visible = (key_labels[None, :] == own_labels[:, None]) & (
        key_place[None, :] <= query_place[:, None]
    )
    soft_scores = (
        jnp.einsum("thd,hud->htu", soft_queries, key_window, preferred_element_type=jnp.float32)
        * scale
    )
    soft_scores = jnp.where(visible[None], soft_scores, -jnp.inf)
    top = jnp.max(soft_scores, axis=-1)
    expo = jnp.exp(soft_scores - top[..., None])
    total = jnp.sum(expo, axis=-1)
    probs = expo / total[..., None]
    probs_half = probs.astype(jnp.bfloat16)
    attended = jnp.einsum(
        "htu,hud->thd", probs_half, value_window, preferred_element_type=jnp.float32
    )
    delta = jnp.sum(as_float(soft_grads) * attended, axis=-1)
    grad_scores = score_grads(probs, soft_grads, value_window, delta)
    soft_query_grad = (
        jnp.einsum("htu,hud->thd", grad_scores, key_window, preferred_element_type=jnp.float32)
        * scale
    )
    key_terms = (
        jnp.einsum("htu,thd->hud", grad_scores, soft_queries, preferred_element_type=jnp.float32)
        * scale
    )
    value_terms = jnp.einsum(
        "htu,thd->hud", probs_half, soft_grads, preferred_element_type=jnp.float32
    )
    soft_key_grad = key_terms[:, (REACH - 1) * tokens :]
    soft_value_grad = value_terms[:, (REACH - 1) * tokens :]
    items = {}
    for back in range(1, REACH):
        lower = (REACH - 1 - back) * tokens
        chain = jnp.prod(behind[REACH - back : REACH - 1], axis=0)
        items[back] = packed(
            key_terms[:, lower : lower + tokens],
            value_terms[:, lower : lower + tokens],
            chain[:, None, None] * back_summary,
        )
    size = items[1].shape[0]

    def wire(value):
        return value.astype(jnp.bfloat16)

    first = as_float(shifted(wire(jnp.concatenate([items[5], items[3], items[1]])), "seq", -1))
    second = as_float(
        shifted(
            wire(jnp.concatenate([items[2] + first[size : 2 * size], items[4] + first[:size]])),
            "seq",
            -2,
        )
    )
    third = as_float(shifted(wire(second[size:]), "seq", -2))
    total = first[2 * size :] + second[:size] + third
    got_key, got_value, reverse_in = unpacked(total, (kv_shape, kv_shape, state_shape))
    soft_key_grad = soft_key_grad + got_key
    soft_value_grad = soft_value_grad + got_value
    lin_key_grad = lin_key_grad + (
        jnp.einsum("she,hde->shd", as_float(values), reverse_in, precision=HIGH_PRECISION)
        * leave.T[:, :, None]
    )
    lin_value_grad = lin_value_grad + (
        jnp.einsum("shd,hde->she", as_float(keys), reverse_in, precision=HIGH_PRECISION)
        * leave.T[:, :, None]
    )

    def merge_heads(array):
        return array.reshape(tokens, heads * HD).astype(jnp.bfloat16)

    return (
        merge_heads(lin_query_grad),
        merge_heads(lin_key_grad),
        merge_heads(lin_value_grad),
        merge_heads(soft_query_grad),
        merge_heads(soft_key_grad.transpose(1, 0, 2)),
        merge_heads(soft_value_grad.transpose(1, 0, 2)),
    )


def split_mesh(mesh):
    count = mesh.shape["tp"]
    inner = math.isqrt(count)
    if inner * inner != count:
        inner = 1
    devices = mesh.devices.reshape(mesh.shape["seq"], count // inner, inner)
    return jax.sharding.Mesh(devices, ("seq",) + TP)


def solution(mesh):
    return jax.shard_map(
        body,
        mesh=split_mesh(mesh),
        in_specs=(
            P("seq", TP),
            P("seq", TP),
            P("seq", TP),
            P(TP),
            P(TP),
            P("seq", TP),
            P("seq", TP),
            P("seq", TP),
            P("seq", TP),
            P("seq", TP),
            P(),
        ),
        out_specs=(
            P("seq", TP),
            P("seq", TP),
            P("seq", TP),
            P("seq", TP),
            P("seq", TP),
            P("seq", TP),
        ),
        check_vma=False,
    )
```

```python
import math

import jax
import jax.numpy as jnp
from jax import lax
from jax.sharding import PartitionSpec as P

HD = 128
BLK = 128
REACH = 6


HIGH_PRECISION = lax.Precision.HIGHEST
NORM_EPS = 1e-06
TP = ("tp_outer", "tp_inner")


def shifted(value, axis, steps):
    count = lax.axis_size(axis)
    first, last = (max(0, -steps), min(count, count - steps))
    return lax.ppermute(value, axis, [(source, source + steps) for source in range(first, last)])


def tp_sum(value, axes):
    for axis in reversed(axes):
        value = jnp.sum(lax.all_gather(value, axis), axis=0)
    return value


def packed(*parts):
    return jnp.concatenate([part.reshape(-1) for part in parts])


def unpacked(flat, shapes):
    out, at = [], 0
    for shape in shapes:
        size = math.prod(shape)
        out.append(flat[at : at + size].reshape(shape))
        at += size
    return out


def as_float(array):
    return array.astype(jnp.float32)


def decay_matrix(labels, decay_rate):
    place = jnp.arange(labels.shape[0], dtype=jnp.int32)
    distance = as_float(place[:, None] - place[None, :])
    visible = (labels[:, None] == labels[None, :]) & (distance >= 0)
    return jnp.where(
        visible[None], jnp.exp(-decay_rate[:, None, None] * jnp.maximum(distance, 0.0)[None]), 0.0
    )


def entry_weights(labels, decay_rate):
    place = as_float(jnp.arange(labels.shape[0], dtype=jnp.int32))
    return jnp.where(
        (labels == labels[:1])[None, :], jnp.exp(-decay_rate[:, None] * place[None, :]), 0.0
    )


def exit_weights(labels, decay_rate):
    count = labels.shape[0]
    place = as_float(jnp.arange(count, dtype=jnp.int32))
    return jnp.where(
        (labels == labels[-1:])[None, :],
        jnp.exp(-decay_rate[:, None] * (count - 1 - place)[None, :]),
        0.0,
    )


def forward_summary(keys, values, labels, link, decay_rate):
    count = labels.shape[0]
    place = as_float(jnp.arange(count, dtype=jnp.int32))
    weight = jnp.where(
        (labels == labels[-1:])[None, :] & link[None, :],
        jnp.exp(-decay_rate[:, None] * (count - place)[None, :]),
        0.0,
    )
    return jnp.einsum(
        "thd,the->hde",
        as_float(keys) * weight.T[:, :, None],
        as_float(values),
        precision=HIGH_PRECISION,
    )


def backward_summary(queries, grads, labels, link, decay_rate):
    count = labels.shape[0]
    place = as_float(jnp.arange(count, dtype=jnp.int32))
    weight = jnp.where(
        (labels == labels[:1])[None, :] & link[None, :],
        jnp.exp(-decay_rate[:, None] * (place + 1.0)[None, :]),
        0.0,
    )
    return jnp.einsum(
        "thd,the->hde",
        as_float(queries) * weight.T[:, :, None],
        as_float(grads),
        precision=HIGH_PRECISION,
    )


def score_grads(probs, grads, value_part, delta):
    grad_probs = jnp.einsum("thd,uhd->htu", grads, value_part, preferred_element_type=jnp.float32)
    return (probs * (grad_probs - delta.T[:, :, None])).astype(jnp.bfloat16)


def body(
    lin_query,
    lin_key,
    lin_value,
    decay_rate,
    norm_gain,
    lin_grad,
    soft_query,
    soft_key,
    soft_value,
    soft_grad,
    segments,
):
    tokens = lin_query.shape[0]
    heads = lin_query.shape[1] // HD
    scale = 1.0 / math.sqrt(HD)
    device = lax.axis_index("seq")
    blocks_each = tokens // BLK
    pad_blocks = REACH * blocks_each
    padded = jnp.concatenate(
        [jnp.full((pad_blocks,), -1, jnp.int32), segments, jnp.full((pad_blocks,), -2, jnp.int32)]
    )
    window_blocks = lax.dynamic_slice_in_dim(
        padded, device * blocks_each, (2 * REACH + 1) * blocks_each
    )
    window_labels = jnp.broadcast_to(window_blocks[:, None], (window_blocks.shape[0], BLK)).reshape(-1)
    own_labels = window_labels[REACH * tokens : (REACH + 1) * tokens]
    key_labels = window_labels[tokens : (REACH + 1) * tokens]

    def split_heads(array):
        return array.reshape(tokens, heads, HD)

    queries = split_heads(lin_query)
    keys = split_heads(lin_key)
    values = split_heads(lin_value)
    soft_queries = split_heads(soft_query)
    soft_keys = split_heads(soft_key)
    soft_values = split_heads(soft_value)
    soft_grads = split_heads(soft_grad)
    span = 2 * REACH + 1
    firsts = window_blocks[::blocks_each]
    lasts = window_blocks[blocks_each - 1 :: blocks_each]
    summary = forward_summary(
        keys, values, own_labels, lasts[REACH : REACH + 1] == firsts[REACH + 1 : REACH + 2], decay_rate
    )
    full_decay = jnp.exp(-decay_rate * tokens)
    ahead = jnp.where((firsts[:-1] == firsts[1:])[:, None], full_decay[None, :], 0.0)
    behind = jnp.where(
        ((firsts[1:] == lasts[:-1]) & (firsts[1:] == lasts[1:]))[:, None], full_decay[None, :], 0.0
    )
    kv_shape = soft_keys.shape
    state_shape = summary.shape
    unit = packed(soft_keys, soft_values, summary.astype(jnp.bfloat16))
    size = unit.shape[0]
    two_back = shifted(unit, "seq", 2)
    odd_back = shifted(jnp.concatenate([unit, two_back]), "seq", 1)
    far_back = shifted(jnp.concatenate([two_back, odd_back[size:]]), "seq", 2)
    arrived = {
        1: odd_back[:size],
        2: two_back,
        3: odd_back[size:],
        4: far_back[:size],
        5: far_back[size:],
    }
    received = []
    state_in = jnp.zeros_like(summary)
    for back in range(1, REACH):
        got_key, got_value, got_state = unpacked(arrived[back], (kv_shape, kv_shape, state_shape))
        received.append((got_key, got_value))
        chain = jnp.prod(ahead[REACH - back + 1 : REACH], axis=0)
        state_in = state_in + chain[:, None, None] * as_float(got_state)
    decay = decay_matrix(own_labels, decay_rate)
    scores = jnp.einsum("thd,shd->hts", queries, keys, preferred_element_type=jnp.float32)
    weights = (decay * scores).astype(jnp.bfloat16)
    entry = entry_weights(own_labels, decay_rate)
    leave = exit_weights(own_labels, decay_rate)
    inner = jnp.einsum("hts,shd->thd", weights, values, preferred_element_type=jnp.float32)
    carried = jnp.einsum("thd,hde->the", as_float(queries), state_in, precision=HIGH_PRECISION)
    lin_out = inner + carried * entry.T[:, :, None]
    flat = lin_out.reshape(tokens, heads * HD)
    scaled_grad = norm_gain[None, :] * as_float(lin_grad)
    sums = tp_sum(jnp.stack([jnp.sum(flat * flat, axis=1), jnp.sum(flat * scaled_grad, axis=1)]), TP)
    width = lax.axis_size(TP) * heads * HD
    inverse = lax.rsqrt(sums[0] / width + NORM_EPS)
    cross = sums[1] / width
    norm_grad = (inverse[:, None] * scaled_grad - flat * (inverse**3 * cross)[:, None]).astype(
        jnp.bfloat16
    )
    grad_heads = split_heads(norm_grad)
    back_summary = backward_summary(
        queries, grad_heads, own_labels, firsts[REACH : REACH + 1] == lasts[REACH - 1 : REACH], decay_rate
    )
    back_state = back_summary.astype(jnp.bfloat16)
    grad_scores_lin = jnp.einsum(
        "thd,shd->hts", grad_heads, values, preferred_element_type=jnp.float32
    )
    grad_weights = (decay * grad_scores_lin).astype(jnp.bfloat16)
    lin_query_grad = jnp.einsum(
        "hts,shd->thd", grad_weights, keys, preferred_element_type=jnp.float32
    )
    lin_query_grad = (
        lin_query_grad
        + jnp.einsum("the,hde->thd", as_float(grad_heads), state_in, precision=HIGH_PRECISION)
        * entry.T[:, :, None]
    )
    lin_key_grad = jnp.einsum(
        "hts,thd->shd", grad_weights, queries, preferred_element_type=jnp.float32
    )

    lin_value_grad = jnp.einsum(
        "hts,the->she", weights, grad_heads, preferred_element_type=jnp.float32
    )

    key_window = jnp.concatenate(
        [received[back - 1][0] for back in range(REACH - 1, 0, -1)] + [soft_keys], 0
    )
    value_window = jnp.concatenate(
        [received[back - 1][1] for back in range(REACH - 1, 0, -1)] + [soft_values], 0
    )
    query_place = jnp.arange(tokens, dtype=jnp.int32)
    key_place = jnp.arange(REACH * tokens, dtype=jnp.int32) - (REACH - 1) * tokens
    visible = (key_labels[None, :] == own_labels[:, None]) & (
        key_place[None, :] <= query_place[:, None]
    )
    soft_scores = (
        jnp.einsum("thd,uhd->htu", soft_queries, key_window, preferred_element_type=jnp.float32)
        * scale
    )
    soft_scores = jnp.where(visible[None], soft_scores, -jnp.inf)
    top = jnp.max(soft_scores, axis=-1)
    expo = jnp.exp(soft_scores - top[..., None])
    total = jnp.sum(expo, axis=-1)
    probs = expo / total[..., None]
    probs_half = probs.astype(jnp.bfloat16)
    attended = jnp.einsum(
        "htu,uhd->thd", probs_half, value_window, preferred_element_type=jnp.float32
    )
    delta = jnp.sum(as_float(soft_grads) * attended, axis=-1)
    grad_scores = score_grads(probs, soft_grads, value_window, delta)
    soft_query_grad = (
        jnp.einsum("htu,uhd->thd", grad_scores, key_window, preferred_element_type=jnp.float32)
        * scale
    )
    key_terms = (
        jnp.einsum("htu,thd->uhd", grad_scores, soft_queries, preferred_element_type=jnp.float32)
        * scale
    )
    value_terms = jnp.einsum(
        "htu,thd->uhd", probs_half, soft_grads, preferred_element_type=jnp.float32
    )
    soft_key_grad = key_terms[(REACH - 1) * tokens :]
    soft_value_grad = value_terms[(REACH - 1) * tokens :]
    items = {}
    for back in range(1, REACH):
        lower = (REACH - 1 - back) * tokens
        chain = jnp.prod(behind[REACH - back : REACH - 1], axis=0)
        items[back] = packed(
            key_terms[lower : lower + tokens],
            value_terms[lower : lower + tokens],
            chain[:, None, None] * back_summary,
        )
    size = items[1].shape[0]

    def wire(value):
        return value.astype(jnp.bfloat16)

    first = as_float(shifted(wire(jnp.concatenate([items[5], items[3], items[1]])), "seq", -1))
    second = as_float(
        shifted(
            wire(jnp.concatenate([items[2] + first[size : 2 * size], items[4] + first[:size]])),
            "seq",
            -2,
        )
    )
    third = as_float(shifted(wire(second[size:]), "seq", -2))
    total = first[2 * size :] + second[:size] + third
    got_key, got_value, reverse_in = unpacked(total, (kv_shape, kv_shape, state_shape))
    soft_key_grad = soft_key_grad + got_key
    soft_value_grad = soft_value_grad + got_value
    lin_key_grad = lin_key_grad + (
        jnp.einsum("she,hde->shd", as_float(values), reverse_in, precision=HIGH_PRECISION)
        * leave.T[:, :, None]
    )
    lin_value_grad = lin_value_grad + (
        jnp.einsum("shd,hde->she", as_float(keys), reverse_in, precision=HIGH_PRECISION)
        * leave.T[:, :, None]
    )

    def merge_heads(array):
        return array.reshape(tokens, heads * HD).astype(jnp.bfloat16)

    return (
        merge_heads(lin_query_grad),
        merge_heads(lin_key_grad),
        merge_heads(lin_value_grad),
        merge_heads(soft_query_grad),
        merge_heads(soft_key_grad),
        merge_heads(soft_value_grad),
    )


def split_mesh(mesh):
    count = mesh.shape["tp"]
    inner = math.isqrt(count)
    if inner * inner != count:
        inner = 1
    devices = mesh.devices.reshape(mesh.shape["seq"], count // inner, inner)
    return jax.sharding.Mesh(devices, ("seq",) + TP)


def solution(mesh):
    return jax.shard_map(
        body,
        mesh=split_mesh(mesh),
        in_specs=(
            P("seq", TP),
            P("seq", TP),
            P("seq", TP),
            P(TP),
            P(TP),
            P("seq", TP),
            P("seq", TP),
            P("seq", TP),
            P("seq", TP),
            P("seq", TP),
            P(),
        ),
        out_specs=(
            P("seq", TP),
            P("seq", TP),
            P("seq", TP),
            P("seq", TP),
            P("seq", TP),
            P("seq", TP),
        ),
        check_vma=False,
    )
```

```python
import math

import jax
import jax.numpy as jnp
from jax import lax
from jax.sharding import PartitionSpec as P

HD = 128
BLK = 128
REACH = 6


HIGH_PRECISION = lax.Precision.HIGHEST
NORM_EPS = 1e-06
TP = ("tp_outer", "tp_inner")


def shifted(value, axis, steps):
    count = lax.axis_size(axis)
    first, last = (max(0, -steps), min(count, count - steps))
    return lax.ppermute(value, axis, [(source, source + steps) for source in range(first, last)])


def tp_sum(value, axes):
    for axis in reversed(axes):
        value = jnp.sum(lax.all_gather(value, axis), axis=0)
    return value


def packed(*parts):
    return jnp.concatenate([part.reshape(-1) for part in parts])


def unpacked(flat, shapes):
    out, at = [], 0
    for shape in shapes:
        size = math.prod(shape)
        out.append(flat[at : at + size].reshape(shape))
        at += size
    return out


def as_float(array):
    return array.astype(jnp.float32)


def decay_matrix(labels, decay_rate):
    place = jnp.arange(labels.shape[0], dtype=jnp.int32)
    distance = as_float(place[:, None] - place[None, :])
    visible = (labels[:, None] == labels[None, :]) & (distance >= 0)
    return jnp.where(
        visible[None], jnp.exp(-decay_rate[:, None, None] * jnp.maximum(distance, 0.0)[None]), 0.0
    )


def entry_weights(mask, decay_rate):
    place = as_float(jnp.arange(mask.shape[0], dtype=jnp.int32))
    return jnp.where(mask[None, :], jnp.exp(-decay_rate[:, None] * place[None, :]), 0.0)


def exit_weights(mask, decay_rate):
    count = mask.shape[0]
    place = as_float(jnp.arange(count, dtype=jnp.int32))
    return jnp.where(
        mask[None, :],
        jnp.exp(-decay_rate[:, None] * (count - 1 - place)[None, :]),
        0.0,
    )


def forward_summary(keys, values, mask, decay_rate):
    count = mask.shape[0]
    place = as_float(jnp.arange(count, dtype=jnp.int32))
    weight = jnp.where(
        mask[None, :],
        jnp.exp(-decay_rate[:, None] * (count - place)[None, :]),
        0.0,
    )
    return jnp.einsum(
        "thd,the->hde",
        as_float(keys) * weight.T[:, :, None],
        as_float(values),
        precision=HIGH_PRECISION,
    )


def backward_summary(queries, grads, mask, decay_rate):
    count = mask.shape[0]
    place = as_float(jnp.arange(count, dtype=jnp.int32))
    weight = jnp.where(
        mask[None, :],
        jnp.exp(-decay_rate[:, None] * (place + 1.0)[None, :]),
        0.0,
    )
    return jnp.einsum(
        "thd,the->hde",
        as_float(queries) * weight.T[:, :, None],
        as_float(grads),
        precision=HIGH_PRECISION,
    )


def score_grads(probs, grads, value_part, delta):
    grad_probs = jnp.einsum("thd,uhd->htu", grads, value_part, preferred_element_type=jnp.float32)
    return (probs * (grad_probs - delta.T[:, :, None])).astype(jnp.bfloat16)


def body(
    lin_query,
    lin_key,
    lin_value,
    decay_rate,
    norm_gain,
    lin_grad,
    soft_query,
    soft_key,
    soft_value,
    soft_grad,
    segments,
):
    tokens = lin_query.shape[0]
    heads = lin_query.shape[1] // HD
    scale = 1.0 / math.sqrt(HD)
    device = lax.axis_index("seq")
    blocks_each = tokens // BLK
    pad_blocks = REACH * blocks_each
    padded = jnp.concatenate(
        [jnp.full((pad_blocks,), -1, jnp.int32), segments, jnp.full((pad_blocks,), -2, jnp.int32)]
    )
    window_blocks = lax.dynamic_slice_in_dim(
        padded, device * blocks_each, (2 * REACH + 1) * blocks_each
    )
    window_labels = lax.optimization_barrier(
        jnp.broadcast_to(window_blocks[:, None], (window_blocks.shape[0], BLK)).reshape(-1)
    )
    own_labels = window_labels[REACH * tokens : (REACH + 1) * tokens]
    key_labels = window_labels[tokens : (REACH + 1) * tokens]

    def split_heads(array):
        return array.reshape(tokens, heads, HD)

    queries = split_heads(lin_query)
    keys = split_heads(lin_key)
    values = split_heads(lin_value)
    soft_queries = split_heads(soft_query)
    soft_keys = split_heads(soft_key)
    soft_values = split_heads(soft_value)
    soft_grads = split_heads(soft_grad)
    span = 2 * REACH + 1
    firsts = window_blocks[::blocks_each]
    lasts = window_blocks[blocks_each - 1 :: blocks_each]
    if blocks_each == 1:
        same_first = same_last = jnp.ones((tokens,), bool)
        same_next = own_labels == window_labels[(REACH + 1) * tokens : (REACH + 2) * tokens]
        same_prev = own_labels == window_labels[(REACH - 1) * tokens : REACH * tokens]
    else:
        same_first = own_labels == own_labels[:1]
        same_last = own_labels == own_labels[-1:]
        same_next = same_last & (lasts[REACH : REACH + 1] == firsts[REACH + 1 : REACH + 2])
        same_prev = same_first & (firsts[REACH : REACH + 1] == lasts[REACH - 1 : REACH])
    summary = forward_summary(keys, values, same_next, decay_rate)
    full_decay = jnp.exp(-decay_rate * tokens)
    ahead = jnp.where((firsts[:-1] == firsts[1:])[:, None], full_decay[None, :], 0.0)
    behind = jnp.where(
        ((firsts[1:] == lasts[:-1]) & (firsts[1:] == lasts[1:]))[:, None], full_decay[None, :], 0.0
    )
    kv_shape = soft_keys.shape
    state_shape = summary.shape
    unit = packed(soft_keys, soft_values, summary.astype(jnp.bfloat16))
    size = unit.shape[0]
    two_back = shifted(unit, "seq", 2)
    four_back = shifted(two_back, "seq", 2)
    odd_back = shifted(jnp.concatenate([unit, two_back]), "seq", 1)
    five_back = shifted(four_back, "seq", 1)
    arrived = {
        1: odd_back[:size],
        2: two_back,
        3: odd_back[size:],
        4: four_back,
        5: five_back,
    }
    received = []
    state_in = jnp.zeros_like(summary)
    for back in range(1, REACH):
        got_key, got_value, got_state = unpacked(arrived[back], (kv_shape, kv_shape, state_shape))
        received.append((got_key, got_value))
        chain = jnp.prod(ahead[REACH - back + 1 : REACH], axis=0)
        state_in = state_in + chain[:, None, None] * as_float(got_state)
    decay = decay_matrix(own_labels, decay_rate)
    scores = jnp.einsum("thd,shd->hts", queries, keys, preferred_element_type=jnp.float32)
    weights = (decay * scores).astype(jnp.bfloat16)
    entry = entry_weights(same_first, decay_rate)
    leave = exit_weights(same_last, decay_rate)
    inner = jnp.einsum("hts,shd->thd", weights, values, preferred_element_type=jnp.float32)
    carried = jnp.einsum("thd,hde->the", as_float(queries), state_in, precision=HIGH_PRECISION)
    lin_out = inner + carried * entry.T[:, :, None]
    flat = lin_out.reshape(tokens, heads * HD)
    scaled_grad = norm_gain[None, :] * as_float(lin_grad)
    sums = tp_sum(jnp.stack([jnp.sum(flat * flat, axis=1), jnp.sum(flat * scaled_grad, axis=1)]), TP)
    width = lax.axis_size(TP) * heads * HD
    inverse = lax.rsqrt(sums[0] / width + NORM_EPS)
    cross = sums[1] / width
    norm_grad = (inverse[:, None] * scaled_grad - flat * (inverse**3 * cross)[:, None]).astype(
        jnp.bfloat16
    )
    grad_heads = split_heads(norm_grad)
    back_summary = backward_summary(queries, grad_heads, same_prev, decay_rate)
    back_state = back_summary.astype(jnp.bfloat16)
    grad_scores_lin = jnp.einsum(
        "thd,shd->hts", grad_heads, values, preferred_element_type=jnp.float32
    )
    grad_weights = (decay * grad_scores_lin).astype(jnp.bfloat16)
    lin_query_grad = jnp.einsum(
        "hts,shd->thd", grad_weights, keys, preferred_element_type=jnp.float32
    )
    lin_query_grad = (
        lin_query_grad
        + jnp.einsum("the,hde->thd", as_float(grad_heads), state_in, precision=HIGH_PRECISION)
        * entry.T[:, :, None]
    )
    lin_key_grad = jnp.einsum(
        "hts,thd->shd", grad_weights, queries, preferred_element_type=jnp.float32
    )

    lin_value_grad = jnp.einsum(
        "hts,the->she", weights, grad_heads, preferred_element_type=jnp.float32
    )

    key_window = jnp.concatenate(
        [received[back - 1][0] for back in range(REACH - 1, 0, -1)] + [soft_keys], 0
    )
    value_window = jnp.concatenate(
        [received[back - 1][1] for back in range(REACH - 1, 0, -1)] + [soft_values], 0
    )
    query_place = jnp.arange(tokens, dtype=jnp.int32)
    key_place = jnp.arange(REACH * tokens, dtype=jnp.int32) - (REACH - 1) * tokens
    visible = (key_labels[None, :] == own_labels[:, None]) & (
        key_place[None, :] <= query_place[:, None]
    )
    soft_scores = (
        jnp.einsum("thd,uhd->htu", soft_queries, key_window, preferred_element_type=jnp.float32)
        * scale
    )
    soft_scores = jnp.where(visible[None], soft_scores, -jnp.inf)
    top = jnp.max(soft_scores, axis=-1)
    expo = jnp.exp(soft_scores - top[..., None])
    total = jnp.sum(expo, axis=-1)
    probs = expo / total[..., None]
    probs_half = probs.astype(jnp.bfloat16)
    attended = jnp.einsum(
        "htu,uhd->thd", probs_half, value_window, preferred_element_type=jnp.float32
    )
    delta = jnp.sum(as_float(soft_grads) * attended, axis=-1)
    grad_scores = score_grads(probs, soft_grads, value_window, delta)
    soft_query_grad = (
        jnp.einsum("htu,uhd->thd", grad_scores, key_window, preferred_element_type=jnp.float32)
        * scale
    )
    key_terms = (
        jnp.einsum("htu,thd->uhd", grad_scores, soft_queries, preferred_element_type=jnp.float32)
        * scale
    )
    value_terms = jnp.einsum(
        "htu,thd->uhd", probs_half, soft_grads, preferred_element_type=jnp.float32
    )
    soft_key_grad = key_terms[(REACH - 1) * tokens :]
    soft_value_grad = value_terms[(REACH - 1) * tokens :]
    items = {}
    for back in range(1, REACH):
        lower = (REACH - 1 - back) * tokens
        chain = jnp.prod(behind[REACH - back : REACH - 1], axis=0)
        items[back] = packed(
            key_terms[lower : lower + tokens],
            value_terms[lower : lower + tokens],
            chain[:, None, None] * back_summary,
        )
    size = items[1].shape[0]

    def wire(value):
        return value.astype(jnp.bfloat16)

    first = as_float(shifted(wire(jnp.concatenate([items[5], items[3], items[1]])), "seq", -1))
    second = as_float(
        shifted(
            wire(jnp.concatenate([items[2] + first[size : 2 * size], items[4] + first[:size]])),
            "seq",
            -2,
        )
    )
    third = as_float(shifted(wire(second[size:]), "seq", -2))
    total = first[2 * size :] + second[:size] + third
    got_key, got_value, reverse_in = unpacked(total, (kv_shape, kv_shape, state_shape))
    soft_key_grad = soft_key_grad + got_key
    soft_value_grad = soft_value_grad + got_value
    lin_key_grad = lin_key_grad + (
        jnp.einsum("she,hde->shd", as_float(values), reverse_in, precision=HIGH_PRECISION)
        * leave.T[:, :, None]
    )
    lin_value_grad = lin_value_grad + (
        jnp.einsum("shd,hde->she", as_float(keys), reverse_in, precision=HIGH_PRECISION)
        * leave.T[:, :, None]
    )

    def merge_heads(array):
        return array.reshape(tokens, heads * HD).astype(jnp.bfloat16)

    return (
        merge_heads(lin_query_grad),
        merge_heads(lin_key_grad),
        merge_heads(lin_value_grad),
        merge_heads(soft_query_grad),
        merge_heads(soft_key_grad),
        merge_heads(soft_value_grad),
    )


def split_mesh(mesh):
    count = mesh.shape["tp"]
    inner = math.isqrt(count)
    if inner * inner != count:
        inner = 1
    devices = mesh.devices.reshape(mesh.shape["seq"], count // inner, inner)
    return jax.sharding.Mesh(devices, ("seq",) + TP)


def solution(mesh):
    return jax.shard_map(
        body,
        mesh=split_mesh(mesh),
        in_specs=(
            P("seq", TP),
            P("seq", TP),
            P("seq", TP),
            P(TP),
            P(TP),
            P("seq", TP),
            P("seq", TP),
            P("seq", TP),
            P("seq", TP),
            P("seq", TP),
            P(),
        ),
        out_specs=(
            P("seq", TP),
            P("seq", TP),
            P("seq", TP),
            P("seq", TP),
            P("seq", TP),
            P("seq", TP),
        ),
        check_vma=False,
    )
```

```python
import math

import jax
import jax.numpy as jnp
from jax import lax
from jax.sharding import PartitionSpec as P

HD = 128
BLK = 128
REACH = 6


HIGH_PRECISION = lax.Precision.HIGHEST
NORM_EPS = 1e-06
TP = ("tp_outer", "tp_inner")


def shifted(value, axis, steps):
    count = lax.axis_size(axis)
    first, last = (max(0, -steps), min(count, count - steps))
    return lax.ppermute(value, axis, [(source, source + steps) for source in range(first, last)])


def tp_sum(value, axes):
    for axis in reversed(axes):
        value = jnp.sum(lax.all_gather(value, axis), axis=0)
    return value


def packed(*parts):
    return jnp.concatenate([part.reshape(-1) for part in parts])


def unpacked(flat, shapes):
    out, at = [], 0
    for shape in shapes:
        size = math.prod(shape)
        out.append(flat[at : at + size].reshape(shape))
        at += size
    return out


def as_float(array):
    return array.astype(jnp.float32)


def decay_matrix(labels, decay_rate):
    place = jnp.arange(labels.shape[0], dtype=jnp.int32)
    distance = as_float(place[:, None] - place[None, :])
    visible = (labels[:, None] == labels[None, :]) & (distance >= 0)
    return jnp.where(
        visible[None], jnp.exp(-decay_rate[:, None, None] * jnp.maximum(distance, 0.0)[None]), 0.0
    )


def entry_weights(mask, decay_rate):
    place = as_float(jnp.arange(mask.shape[0], dtype=jnp.int32))
    return jnp.where(mask[None, :], jnp.exp(-decay_rate[:, None] * place[None, :]), 0.0)


def exit_weights(mask, decay_rate):
    count = mask.shape[0]
    place = as_float(jnp.arange(count, dtype=jnp.int32))
    return jnp.where(
        mask[None, :],
        jnp.exp(-decay_rate[:, None] * (count - 1 - place)[None, :]),
        0.0,
    )


def forward_summary(keys, values, mask, decay_rate):
    count = mask.shape[0]
    place = as_float(jnp.arange(count, dtype=jnp.int32))
    weight = jnp.where(
        mask[None, :],
        jnp.exp(-decay_rate[:, None] * (count - place)[None, :]),
        0.0,
    )
    return jnp.einsum(
        "thd,the->hde",
        as_float(keys) * weight.T[:, :, None],
        as_float(values),
        precision=HIGH_PRECISION,
    )


def backward_summary(queries, grads, mask, decay_rate):
    count = mask.shape[0]
    place = as_float(jnp.arange(count, dtype=jnp.int32))
    weight = jnp.where(
        mask[None, :],
        jnp.exp(-decay_rate[:, None] * (place + 1.0)[None, :]),
        0.0,
    )
    return jnp.einsum(
        "thd,the->hde",
        as_float(queries) * weight.T[:, :, None],
        as_float(grads),
        precision=HIGH_PRECISION,
    )


def score_grads(probs, grads, value_part, delta):
    grad_probs = jnp.einsum("thd,uhd->htu", grads, value_part, preferred_element_type=jnp.float32)
    return (probs * (grad_probs - delta.T[:, :, None])).astype(jnp.bfloat16)


def body(
    lin_query,
    lin_key,
    lin_value,
    decay_rate,
    norm_gain,
    lin_grad,
    soft_query,
    soft_key,
    soft_value,
    soft_grad,
    segments,
):
    tokens = lin_query.shape[0]
    heads = lin_query.shape[1] // HD
    scale = 1.0 / math.sqrt(HD)
    device = lax.axis_index("seq")
    blocks_each = tokens // BLK
    pad_blocks = REACH * blocks_each
    padded = jnp.concatenate(
        [jnp.full((pad_blocks,), -1, jnp.int32), segments, jnp.full((pad_blocks,), -2, jnp.int32)]
    )
    window_blocks = lax.dynamic_slice_in_dim(
        padded, device * blocks_each, (2 * REACH + 1) * blocks_each
    )
    window_labels = lax.optimization_barrier(
        jnp.broadcast_to(window_blocks[:, None], (window_blocks.shape[0], BLK)).reshape(-1)
    )
    own_labels = window_labels[REACH * tokens : (REACH + 1) * tokens]
    key_labels = window_labels[tokens : (REACH + 1) * tokens]

    def split_heads(array):
        return array.reshape(tokens, heads, HD)

    queries = split_heads(lin_query)
    keys = split_heads(lin_key)
    values = split_heads(lin_value)
    soft_queries = split_heads(soft_query)
    soft_keys = split_heads(soft_key)
    soft_values = split_heads(soft_value)
    soft_grads = split_heads(soft_grad)
    span = 2 * REACH + 1
    firsts = window_blocks[::blocks_each]
    lasts = window_blocks[blocks_each - 1 :: blocks_each]
    if blocks_each == 1:
        same_first = same_last = jnp.ones((tokens,), bool)
        same_next = own_labels == window_labels[(REACH + 1) * tokens : (REACH + 2) * tokens]
        same_prev = own_labels == window_labels[(REACH - 1) * tokens : REACH * tokens]
    else:
        same_first = own_labels == own_labels[:1]
        same_last = own_labels == own_labels[-1:]
        same_next = same_last & (lasts[REACH : REACH + 1] == firsts[REACH + 1 : REACH + 2])
        same_prev = same_first & (firsts[REACH : REACH + 1] == lasts[REACH - 1 : REACH])
    summary = forward_summary(keys, values, same_next, decay_rate)
    full_decay = jnp.exp(-decay_rate * tokens)
    ahead = jnp.where((firsts[:-1] == firsts[1:])[:, None], full_decay[None, :], 0.0)
    behind = jnp.where(
        ((firsts[1:] == lasts[:-1]) & (firsts[1:] == lasts[1:]))[:, None], full_decay[None, :], 0.0
    )
    kv_shape = soft_keys.shape
    state_shape = summary.shape
    unit = packed(soft_keys, soft_values, summary.astype(jnp.bfloat16))
    size = unit.shape[0]
    two_back = shifted(unit, "seq", 2)
    four_back = shifted(two_back, "seq", 2)
    odd_back = shifted(jnp.concatenate([unit, two_back]), "seq", 1)
    five_back = shifted(two_back, "seq", 3)
    arrived = {
        1: odd_back[:size],
        2: two_back,
        3: odd_back[size:],
        4: four_back,
        5: five_back,
    }
    received = []
    state_in = jnp.zeros_like(summary)
    for back in range(1, REACH):
        got_key, got_value, got_state = unpacked(arrived[back], (kv_shape, kv_shape, state_shape))
        received.append((got_key, got_value))
        chain = jnp.prod(ahead[REACH - back + 1 : REACH], axis=0)
        state_in = state_in + chain[:, None, None] * as_float(got_state)
    decay = decay_matrix(own_labels, decay_rate)
    scores = jnp.einsum("thd,shd->hts", queries, keys, preferred_element_type=jnp.float32)
    weights = (decay * scores).astype(jnp.bfloat16)
    entry = entry_weights(same_first, decay_rate)
    leave = exit_weights(same_last, decay_rate)
    inner = jnp.einsum("hts,shd->thd", weights, values, preferred_element_type=jnp.float32)
    carried = jnp.einsum("thd,hde->the", as_float(queries), state_in, precision=HIGH_PRECISION)
    lin_out = inner + carried * entry.T[:, :, None]
    flat = lin_out.reshape(tokens, heads * HD)
    scaled_grad = norm_gain[None, :] * as_float(lin_grad)
    sums = tp_sum(jnp.stack([jnp.sum(flat * flat, axis=1), jnp.sum(flat * scaled_grad, axis=1)]), TP)
    width = lax.axis_size(TP) * heads * HD
    inverse = lax.rsqrt(sums[0] / width + NORM_EPS)
    cross = sums[1] / width
    norm_grad = (inverse[:, None] * scaled_grad - flat * (inverse**3 * cross)[:, None]).astype(
        jnp.bfloat16
    )
    grad_heads = split_heads(norm_grad)
    back_summary = backward_summary(queries, grad_heads, same_prev, decay_rate)
    back_state = back_summary.astype(jnp.bfloat16)
    grad_scores_lin = jnp.einsum(
        "thd,shd->hts", grad_heads, values, preferred_element_type=jnp.float32
    )
    grad_weights = (decay * grad_scores_lin).astype(jnp.bfloat16)
    lin_query_grad = jnp.einsum(
        "hts,shd->thd", grad_weights, keys, preferred_element_type=jnp.float32
    )
    lin_query_grad = (
        lin_query_grad
        + jnp.einsum("the,hde->thd", as_float(grad_heads), state_in, precision=HIGH_PRECISION)
        * entry.T[:, :, None]
    )
    lin_key_grad = jnp.einsum(
        "hts,thd->shd", grad_weights, queries, preferred_element_type=jnp.float32
    )

    lin_value_grad = jnp.einsum(
        "hts,the->she", weights, grad_heads, preferred_element_type=jnp.float32
    )

    key_window = jnp.concatenate(
        [received[back - 1][0] for back in range(REACH - 1, 0, -1)] + [soft_keys], 0
    )
    value_window = jnp.concatenate(
        [received[back - 1][1] for back in range(REACH - 1, 0, -1)] + [soft_values], 0
    )
    query_place = jnp.arange(tokens, dtype=jnp.int32)
    key_place = jnp.arange(REACH * tokens, dtype=jnp.int32) - (REACH - 1) * tokens
    visible = (key_labels[None, :] == own_labels[:, None]) & (
        key_place[None, :] <= query_place[:, None]
    )
    soft_scores = (
        jnp.einsum("thd,uhd->htu", soft_queries, key_window, preferred_element_type=jnp.float32)
        * scale
    )
    soft_scores = jnp.where(visible[None], soft_scores, -jnp.inf)
    top = jnp.max(soft_scores, axis=-1)
    expo = jnp.exp(soft_scores - top[..., None])
    total = jnp.sum(expo, axis=-1)
    probs = expo / total[..., None]
    probs_half = probs.astype(jnp.bfloat16)
    attended = jnp.einsum(
        "htu,uhd->thd", probs_half, value_window, preferred_element_type=jnp.float32
    )
    delta = jnp.sum(as_float(soft_grads) * attended, axis=-1)
    grad_scores = score_grads(probs, soft_grads, value_window, delta)
    soft_query_grad = (
        jnp.einsum("htu,uhd->thd", grad_scores, key_window, preferred_element_type=jnp.float32)
        * scale
    )
    key_terms = (
        jnp.einsum("htu,thd->uhd", grad_scores, soft_queries, preferred_element_type=jnp.float32)
        * scale
    )
    value_terms = jnp.einsum(
        "htu,thd->uhd", probs_half, soft_grads, preferred_element_type=jnp.float32
    )
    soft_key_grad = key_terms[(REACH - 1) * tokens :]
    soft_value_grad = value_terms[(REACH - 1) * tokens :]
    items = {}
    for back in range(1, REACH):
        lower = (REACH - 1 - back) * tokens
        chain = jnp.prod(behind[REACH - back : REACH - 1], axis=0)
        items[back] = packed(
            key_terms[lower : lower + tokens],
            value_terms[lower : lower + tokens],
            chain[:, None, None] * back_summary,
        )
    size = items[1].shape[0]

    def wire(value):
        return value.astype(jnp.bfloat16)

    first = as_float(shifted(wire(jnp.concatenate([items[5], items[3], items[1]])), "seq", -1))
    second = as_float(
        shifted(
            wire(jnp.concatenate([items[2] + first[size : 2 * size], items[4] + first[:size]])),
            "seq",
            -2,
        )
    )
    third = as_float(shifted(wire(second[size:]), "seq", -2))
    total = first[2 * size :] + second[:size] + third
    got_key, got_value, reverse_in = unpacked(total, (kv_shape, kv_shape, state_shape))
    soft_key_grad = soft_key_grad + got_key
    soft_value_grad = soft_value_grad + got_value
    lin_key_grad = lin_key_grad + (
        jnp.einsum("she,hde->shd", as_float(values), reverse_in, precision=HIGH_PRECISION)
        * leave.T[:, :, None]
    )
    lin_value_grad = lin_value_grad + (
        jnp.einsum("shd,hde->she", as_float(keys), reverse_in, precision=HIGH_PRECISION)
        * leave.T[:, :, None]
    )

    def merge_heads(array):
        return array.reshape(tokens, heads * HD).astype(jnp.bfloat16)

    return (
        merge_heads(lin_query_grad),
        merge_heads(lin_key_grad),
        merge_heads(lin_value_grad),
        merge_heads(soft_query_grad),
        merge_heads(soft_key_grad),
        merge_heads(soft_value_grad),
    )


def split_mesh(mesh):
    count = mesh.shape["tp"]
    inner = math.isqrt(count)
    if inner * inner != count:
        inner = 1
    devices = mesh.devices.reshape(mesh.shape["seq"], count // inner, inner)
    return jax.sharding.Mesh(devices, ("seq",) + TP)


def solution(mesh):
    return jax.shard_map(
        body,
        mesh=split_mesh(mesh),
        in_specs=(
            P("seq", TP),
            P("seq", TP),
            P("seq", TP),
            P(TP),
            P(TP),
            P("seq", TP),
            P("seq", TP),
            P("seq", TP),
            P("seq", TP),
            P("seq", TP),
            P(),
        ),
        out_specs=(
            P("seq", TP),
            P("seq", TP),
            P("seq", TP),
            P("seq", TP),
            P("seq", TP),
            P("seq", TP),
        ),
        check_vma=False,
    )
```

```python
import math

import jax
import jax.numpy as jnp
from jax import lax
from jax.sharding import PartitionSpec as P

HD = 128
BLK = 128
REACH = 6


HIGH_PRECISION = lax.Precision.HIGHEST
NORM_EPS = 1e-06
TP = ("tp_outer", "tp_inner")


def shifted(value, axis, steps):
    count = lax.axis_size(axis)
    first, last = (max(0, -steps), min(count, count - steps))
    return lax.ppermute(value, axis, [(source, source + steps) for source in range(first, last)])


def tp_sum(value, axes):
    for axis in reversed(axes):
        value = jnp.sum(lax.all_gather(value, axis), axis=0)
    return value


def packed(*parts):
    return jnp.concatenate([part.reshape(-1) for part in parts])


def unpacked(flat, shapes):
    out, at = [], 0
    for shape in shapes:
        size = math.prod(shape)
        out.append(flat[at : at + size].reshape(shape))
        at += size
    return out


def as_float(array):
    return array.astype(jnp.float32)


def decay_matrix(labels, decay_rate):
    place = jnp.arange(labels.shape[0], dtype=jnp.int32)
    distance = as_float(place[:, None] - place[None, :])
    visible = (labels[:, None] == labels[None, :]) & (distance >= 0)
    return jnp.where(
        visible[None], jnp.exp(-decay_rate[:, None, None] * jnp.maximum(distance, 0.0)[None]), 0.0
    )


def entry_weights(mask, decay_rate):
    place = as_float(jnp.arange(mask.shape[0], dtype=jnp.int32))
    return jnp.where(mask[None, :], jnp.exp(-decay_rate[:, None] * place[None, :]), 0.0)


def exit_weights(mask, decay_rate):
    count = mask.shape[0]
    place = as_float(jnp.arange(count, dtype=jnp.int32))
    return jnp.where(
        mask[None, :],
        jnp.exp(-decay_rate[:, None] * (count - 1 - place)[None, :]),
        0.0,
    )


def forward_summary(keys, values, mask, decay_rate):
    count = mask.shape[0]
    place = as_float(jnp.arange(count, dtype=jnp.int32))
    weight = jnp.where(
        mask[None, :],
        jnp.exp(-decay_rate[:, None] * (count - place)[None, :]),
        0.0,
    )
    return jnp.einsum(
        "thd,the->hde",
        as_float(keys) * weight.T[:, :, None],
        as_float(values),
        precision=HIGH_PRECISION,
    )


def backward_summary(queries, grads, mask, decay_rate):
    count = mask.shape[0]
    place = as_float(jnp.arange(count, dtype=jnp.int32))
    weight = jnp.where(
        mask[None, :],
        jnp.exp(-decay_rate[:, None] * (place + 1.0)[None, :]),
        0.0,
    )
    return jnp.einsum(
        "thd,the->hde",
        as_float(queries) * weight.T[:, :, None],
        as_float(grads),
        precision=HIGH_PRECISION,
    )


def score_grads(probs, grads, value_part, delta):
    grad_probs = jnp.einsum("thd,uhd->htu", grads, value_part, preferred_element_type=jnp.float32)
    return (probs * (grad_probs - delta.T[:, :, None])).astype(jnp.bfloat16)


def body(
    lin_query,
    lin_key,
    lin_value,
    decay_rate,
    norm_gain,
    lin_grad,
    soft_query,
    soft_key,
    soft_value,
    soft_grad,
    segments,
):
    tokens = lin_query.shape[0]
    heads = lin_query.shape[1] // HD
    scale = 1.0 / math.sqrt(HD)
    device = lax.axis_index("seq")
    blocks_each = tokens // BLK
    pad_blocks = REACH * blocks_each
    padded = jnp.concatenate(
        [jnp.full((pad_blocks,), -1, jnp.int32), segments, jnp.full((pad_blocks,), -2, jnp.int32)]
    )
    window_blocks = lax.dynamic_slice_in_dim(
        padded, device * blocks_each, (2 * REACH + 1) * blocks_each
    )
    window_labels = lax.optimization_barrier(
        jnp.broadcast_to(window_blocks[:, None], (window_blocks.shape[0], BLK)).reshape(-1)
    )
    own_labels = window_labels[REACH * tokens : (REACH + 1) * tokens]
    key_labels = window_labels[tokens : (REACH + 1) * tokens]

    def split_heads(array):
        return array.reshape(tokens, heads, HD)

    queries = split_heads(lin_query)
    keys = split_heads(lin_key)
    values = split_heads(lin_value)
    soft_queries = split_heads(soft_query)
    soft_keys = split_heads(soft_key)
    soft_values = split_heads(soft_value)
    soft_grads = split_heads(soft_grad)
    span = 2 * REACH + 1
    firsts = window_blocks[::blocks_each]
    lasts = window_blocks[blocks_each - 1 :: blocks_each]
    if blocks_each == 1:
        same_first = same_last = jnp.ones((tokens,), bool)
        same_next = own_labels == window_labels[(REACH + 1) * tokens : (REACH + 2) * tokens]
        same_prev = own_labels == window_labels[(REACH - 1) * tokens : REACH * tokens]
    else:
        same_first = own_labels == own_labels[:1]
        same_last = own_labels == own_labels[-1:]
        same_next = same_last & (lasts[REACH : REACH + 1] == firsts[REACH + 1 : REACH + 2])
        same_prev = same_first & (firsts[REACH : REACH + 1] == lasts[REACH - 1 : REACH])
    summary = forward_summary(keys, values, same_next, decay_rate)
    full_decay = jnp.exp(-decay_rate * tokens)
    ahead = jnp.where((firsts[:-1] == firsts[1:])[:, None], full_decay[None, :], 0.0)
    behind = jnp.where(
        ((firsts[1:] == lasts[:-1]) & (firsts[1:] == lasts[1:]))[:, None], full_decay[None, :], 0.0
    )
    kv_shape = soft_keys.shape
    state_shape = summary.shape
    unit = packed(soft_keys, soft_values, summary.astype(jnp.bfloat16))
    size = unit.shape[0]
    two_back = shifted(unit, "seq", 2)
    four_back = shifted(two_back, "seq", 2)
    odd_back = shifted(jnp.concatenate([unit, two_back]), "seq", 1)
    five_back = shifted(two_back, "seq", 3)
    arrived = {
        1: odd_back[:size],
        2: two_back,
        3: odd_back[size:],
        4: four_back,
        5: five_back,
    }
    received = []
    state_in = jnp.zeros_like(summary)
    for back in range(1, REACH):
        got_key, got_value, got_state = unpacked(arrived[back], (kv_shape, kv_shape, state_shape))
        received.append((got_key, got_value))
        chain = jnp.prod(ahead[REACH - back + 1 : REACH], axis=0)
        state_in = state_in + chain[:, None, None] * as_float(got_state)
    decay = decay_matrix(own_labels, decay_rate)
    scores = jnp.einsum("thd,shd->hts", queries, keys, preferred_element_type=jnp.float32)
    weights = (decay * scores).astype(jnp.bfloat16)
    entry = entry_weights(same_first, decay_rate)
    leave = exit_weights(same_last, decay_rate)
    inner = jnp.einsum("hts,shd->thd", weights, values, preferred_element_type=jnp.float32)
    carried = jnp.einsum("thd,hde->the", as_float(queries), state_in, precision=HIGH_PRECISION)
    lin_out = inner + carried * entry.T[:, :, None]
    flat = lin_out.reshape(tokens, heads * HD)
    scaled_grad = norm_gain[None, :] * as_float(lin_grad)
    sums = tp_sum(jnp.stack([jnp.sum(flat * flat, axis=1), jnp.sum(flat * scaled_grad, axis=1)]), TP)
    width = lax.axis_size(TP) * heads * HD
    inverse = lax.rsqrt(sums[0] / width + NORM_EPS)
    cross = sums[1] / width
    norm_grad = (inverse[:, None] * scaled_grad - flat * (inverse**3 * cross)[:, None]).astype(
        jnp.bfloat16
    )
    grad_heads = split_heads(norm_grad)
    back_summary = backward_summary(queries, grad_heads, same_prev, decay_rate)
    back_state = back_summary.astype(jnp.bfloat16)
    grad_scores_lin = jnp.einsum(
        "thd,shd->hts", grad_heads, values, preferred_element_type=jnp.float32
    )
    grad_weights = (decay * grad_scores_lin).astype(jnp.bfloat16)
    lin_query_grad = jnp.einsum(
        "hts,shd->thd", grad_weights, keys, preferred_element_type=jnp.float32
    )
    lin_query_grad = (
        lin_query_grad
        + jnp.einsum("the,hde->thd", as_float(grad_heads), state_in, precision=HIGH_PRECISION)
        * entry.T[:, :, None]
    )
    lin_key_grad = jnp.einsum(
        "hts,thd->shd", grad_weights, queries, preferred_element_type=jnp.float32
    )

    lin_value_grad = jnp.einsum(
        "hts,the->she", weights, grad_heads, preferred_element_type=jnp.float32
    )

    key_window = jnp.concatenate(
        [received[back - 1][0] for back in range(REACH - 1, 0, -1)] + [soft_keys], 0
    )
    value_window = jnp.concatenate(
        [received[back - 1][1] for back in range(REACH - 1, 0, -1)] + [soft_values], 0
    )
    query_place = jnp.arange(tokens, dtype=jnp.int32)
    key_place = jnp.arange(REACH * tokens, dtype=jnp.int32) - (REACH - 1) * tokens
    visible = (key_labels[None, :] == own_labels[:, None]) & (
        key_place[None, :] <= query_place[:, None]
    )
    soft_scores = (
        jnp.einsum("thd,uhd->htu", soft_queries, key_window, preferred_element_type=jnp.float32)
        * scale
    )
    soft_scores = jnp.where(visible[None], soft_scores, -jnp.inf)
    top = jnp.max(soft_scores, axis=-1)
    expo = jnp.exp(soft_scores - top[..., None])
    total = jnp.sum(expo, axis=-1)
    probs = expo / total[..., None]
    probs_half = probs.astype(jnp.bfloat16)
    attended = jnp.einsum(
        "htu,uhd->thd", probs_half, value_window, preferred_element_type=jnp.float32
    )
    delta = jnp.sum(as_float(soft_grads) * attended, axis=-1)
    grad_scores = score_grads(probs, soft_grads, value_window, delta)
    soft_query_grad = (
        jnp.einsum("htu,uhd->thd", grad_scores, key_window, preferred_element_type=jnp.float32)
        * scale
    )
    key_terms = (
        jnp.einsum("htu,thd->uhd", grad_scores, soft_queries, preferred_element_type=jnp.float32)
        * scale
    )
    value_terms = jnp.einsum(
        "htu,thd->uhd", probs_half, soft_grads, preferred_element_type=jnp.float32
    )
    soft_key_grad = key_terms[(REACH - 1) * tokens :]
    soft_value_grad = value_terms[(REACH - 1) * tokens :]
    items = {}
    for back in range(1, REACH):
        lower = (REACH - 1 - back) * tokens
        chain = jnp.prod(behind[REACH - back : REACH - 1], axis=0)
        items[back] = packed(
            key_terms[lower : lower + tokens],
            value_terms[lower : lower + tokens],
            chain[:, None, None] * back_summary,
        )
    size = items[1].shape[0]

    def wire(value):
        return value.astype(jnp.bfloat16)

    first = as_float(shifted(wire(jnp.concatenate([items[1], items[3], items[4]])), "seq", -1))
    second = as_float(shifted(wire(jnp.concatenate([items[2], items[5]])), "seq", -2))
    third = as_float(shifted(wire(first[size : 2 * size]), "seq", -2))
    fourth = as_float(
        shifted(wire(first[2 * size :] + second[size:]), "seq", -3)
    )
    total = first[:size] + second[:size] + third + fourth
    got_key, got_value, reverse_in = unpacked(total, (kv_shape, kv_shape, state_shape))
    soft_key_grad = soft_key_grad + got_key
    soft_value_grad = soft_value_grad + got_value
    lin_key_grad = lin_key_grad + (
        jnp.einsum("she,hde->shd", as_float(values), reverse_in, precision=HIGH_PRECISION)
        * leave.T[:, :, None]
    )
    lin_value_grad = lin_value_grad + (
        jnp.einsum("shd,hde->she", as_float(keys), reverse_in, precision=HIGH_PRECISION)
        * leave.T[:, :, None]
    )

    def merge_heads(array):
        return array.reshape(tokens, heads * HD).astype(jnp.bfloat16)

    return (
        merge_heads(lin_query_grad),
        merge_heads(lin_key_grad),
        merge_heads(lin_value_grad),
        merge_heads(soft_query_grad),
        merge_heads(soft_key_grad),
        merge_heads(soft_value_grad),
    )


def split_mesh(mesh):
    count = mesh.shape["tp"]
    inner = math.isqrt(count)
    if inner * inner != count:
        inner = 1
    devices = mesh.devices.reshape(mesh.shape["seq"], count // inner, inner)
    return jax.sharding.Mesh(devices, ("seq",) + TP)


def solution(mesh):
    return jax.shard_map(
        body,
        mesh=split_mesh(mesh),
        in_specs=(
            P("seq", TP),
            P("seq", TP),
            P("seq", TP),
            P(TP),
            P(TP),
            P("seq", TP),
            P("seq", TP),
            P("seq", TP),
            P("seq", TP),
            P("seq", TP),
            P(),
        ),
        out_specs=(
            P("seq", TP),
            P("seq", TP),
            P("seq", TP),
            P("seq", TP),
            P("seq", TP),
            P("seq", TP),
        ),
        check_vma=False,
    )
```

```python
import math

import jax
import jax.numpy as jnp
from jax import lax
from jax.experimental.layout import Layout, with_layout_constraint
from jax.sharding import PartitionSpec as P

HD = 128
BLK = 128
REACH = 6


HIGH_PRECISION = lax.Precision.HIGHEST
NORM_EPS = 1e-06
TP = ("tp_outer", "tp_inner")


def shifted(value, axis, steps):
    count = lax.axis_size(axis)
    first, last = (max(0, -steps), min(count, count - steps))
    return lax.ppermute(value, axis, [(source, source + steps) for source in range(first, last)])


def tp_sum(value, axes):
    for axis in reversed(axes):
        value = jnp.sum(lax.all_gather(value, axis), axis=0)
    return value


def packed(*parts):
    return jnp.concatenate([part.reshape(-1) for part in parts])


def unpacked(flat, shapes):
    out, at = [], 0
    for shape in shapes:
        size = math.prod(shape)
        out.append(flat[at : at + size].reshape(shape))
        at += size
    return out


def as_float(array):
    return array.astype(jnp.float32)


def decay_matrix(labels, decay_rate):
    place = jnp.arange(labels.shape[0], dtype=jnp.int32)
    distance = as_float(place[:, None] - place[None, :])
    visible = (labels[:, None] == labels[None, :]) & (distance >= 0)
    return jnp.where(
        visible[None], jnp.exp(-decay_rate[:, None, None] * jnp.maximum(distance, 0.0)[None]), 0.0
    )


def entry_weights(mask, decay_rate):
    place = as_float(jnp.arange(mask.shape[0], dtype=jnp.int32))
    return jnp.where(mask[None, :], jnp.exp(-decay_rate[:, None] * place[None, :]), 0.0)


def exit_weights(mask, decay_rate):
    count = mask.shape[0]
    place = as_float(jnp.arange(count, dtype=jnp.int32))
    return jnp.where(
        mask[None, :],
        jnp.exp(-decay_rate[:, None] * (count - 1 - place)[None, :]),
        0.0,
    )


def forward_summary(keys, values, mask, decay_rate):
    count = mask.shape[0]
    place = as_float(jnp.arange(count, dtype=jnp.int32))
    weight = jnp.where(
        mask[None, :],
        jnp.exp(-decay_rate[:, None] * (count - place)[None, :]),
        0.0,
    )
    return jnp.einsum(
        "thd,the->hde",
        as_float(keys) * weight.T[:, :, None],
        as_float(values),
        precision=HIGH_PRECISION,
    )


def backward_summary(queries, grads, mask, decay_rate):
    count = mask.shape[0]
    place = as_float(jnp.arange(count, dtype=jnp.int32))
    weight = jnp.where(
        mask[None, :],
        jnp.exp(-decay_rate[:, None] * (place + 1.0)[None, :]),
        0.0,
    )
    return jnp.einsum(
        "thd,the->hde",
        as_float(queries) * weight.T[:, :, None],
        as_float(grads),
        precision=HIGH_PRECISION,
    )


def score_grads(probs, grads, value_part, delta):
    grad_probs = jnp.einsum("thd,uhd->htu", grads, value_part, preferred_element_type=jnp.float32)
    return (probs * (grad_probs - delta.T[:, :, None])).astype(jnp.bfloat16)


def body(
    lin_query,
    lin_key,
    lin_value,
    decay_rate,
    norm_gain,
    lin_grad,
    soft_query,
    soft_key,
    soft_value,
    soft_grad,
    segments,
):
    tokens = lin_query.shape[0]
    heads = lin_query.shape[1] // HD
    scale = 1.0 / math.sqrt(HD)
    device = lax.axis_index("seq")
    blocks_each = tokens // BLK
    pad_blocks = REACH * blocks_each
    padded = jnp.concatenate(
        [jnp.full((pad_blocks,), -1, jnp.int32), segments, jnp.full((pad_blocks,), -2, jnp.int32)]
    )
    window_blocks = lax.dynamic_slice_in_dim(
        padded, device * blocks_each, (2 * REACH + 1) * blocks_each
    )
    window_labels = lax.optimization_barrier(
        jnp.broadcast_to(window_blocks[:, None], (window_blocks.shape[0], BLK)).reshape(-1)
    )
    own_labels = window_labels[REACH * tokens : (REACH + 1) * tokens]
    key_labels = window_labels[tokens : (REACH + 1) * tokens]

    def split_heads(array):
        return array.reshape(tokens, heads, HD)

    queries = split_heads(lin_query)
    keys = split_heads(lin_key)
    values = split_heads(lin_value)
    soft_queries = split_heads(soft_query)
    soft_keys = split_heads(soft_key)
    soft_values = split_heads(soft_value)
    soft_grads = split_heads(soft_grad)
    span = 2 * REACH + 1
    firsts = window_blocks[::blocks_each]
    lasts = window_blocks[blocks_each - 1 :: blocks_each]
    if blocks_each == 1:
        same_first = same_last = jnp.ones((tokens,), bool)
        same_next = own_labels == window_labels[(REACH + 1) * tokens : (REACH + 2) * tokens]
        same_prev = own_labels == window_labels[(REACH - 1) * tokens : REACH * tokens]
    else:
        same_first = own_labels == own_labels[:1]
        same_last = own_labels == own_labels[-1:]
        same_next = same_last & (lasts[REACH : REACH + 1] == firsts[REACH + 1 : REACH + 2])
        same_prev = same_first & (firsts[REACH : REACH + 1] == lasts[REACH - 1 : REACH])
    summary = forward_summary(keys, values, same_next, decay_rate)
    full_decay = jnp.exp(-decay_rate * tokens)
    ahead = jnp.where((firsts[:-1] == firsts[1:])[:, None], full_decay[None, :], 0.0)
    behind = jnp.where(
        ((firsts[1:] == lasts[:-1]) & (firsts[1:] == lasts[1:]))[:, None], full_decay[None, :], 0.0
    )
    kv_shape = soft_keys.shape
    state_shape = summary.shape
    unit = packed(soft_keys, soft_values, summary.astype(jnp.bfloat16))
    size = unit.shape[0]
    two_back = shifted(unit, "seq", 2)
    four_back = shifted(two_back, "seq", 2)
    odd_back = shifted(jnp.concatenate([unit, two_back]), "seq", 1)
    five_back = shifted(two_back, "seq", 3)
    arrived = {
        1: odd_back[:size],
        2: two_back,
        3: odd_back[size:],
        4: four_back,
        5: five_back,
    }
    received = []
    state_in = jnp.zeros_like(summary)
    for back in range(1, REACH):
        got_key, got_value, got_state = unpacked(arrived[back], (kv_shape, kv_shape, state_shape))
        received.append((got_key, got_value))
        chain = jnp.prod(ahead[REACH - back + 1 : REACH], axis=0)
        state_in = state_in + chain[:, None, None] * as_float(got_state)
    decay = decay_matrix(own_labels, decay_rate)
    scores = jnp.einsum("thd,shd->hts", queries, keys, preferred_element_type=jnp.float32)
    weights = (decay * scores).astype(jnp.bfloat16)
    entry = entry_weights(same_first, decay_rate)
    leave = exit_weights(same_last, decay_rate)
    inner = jnp.einsum("hts,shd->thd", weights, values, preferred_element_type=jnp.float32)
    carried = jnp.einsum("thd,hde->the", as_float(queries), state_in, precision=HIGH_PRECISION)
    lin_out = inner + carried * entry.T[:, :, None]
    flat = lin_out.reshape(tokens, heads * HD)
    scaled_grad = norm_gain[None, :] * as_float(lin_grad)
    sums = tp_sum(jnp.stack([jnp.sum(flat * flat, axis=1), jnp.sum(flat * scaled_grad, axis=1)]), TP)
    width = lax.axis_size(TP) * heads * HD
    inverse = lax.rsqrt(sums[0] / width + NORM_EPS)
    cross = sums[1] / width
    norm_grad = (inverse[:, None] * scaled_grad - flat * (inverse**3 * cross)[:, None]).astype(
        jnp.bfloat16
    )
    grad_heads = split_heads(norm_grad)
    back_summary = backward_summary(queries, grad_heads, same_prev, decay_rate)
    back_state = back_summary.astype(jnp.bfloat16)
    grad_scores_lin = jnp.einsum(
        "thd,shd->hts", grad_heads, values, preferred_element_type=jnp.float32
    )
    grad_weights = (decay * grad_scores_lin).astype(jnp.bfloat16)
    lin_query_grad = jnp.einsum(
        "hts,shd->thd", grad_weights, keys, preferred_element_type=jnp.float32
    )
    lin_query_grad = (
        lin_query_grad
        + jnp.einsum("the,hde->thd", as_float(grad_heads), state_in, precision=HIGH_PRECISION)
        * entry.T[:, :, None]
    )
    lin_key_grad = jnp.einsum(
        "hts,thd->shd", grad_weights, queries, preferred_element_type=jnp.float32
    )

    lin_value_grad = jnp.einsum(
        "hts,the->she", weights, grad_heads, preferred_element_type=jnp.float32
    )

    key_window = jnp.concatenate(
        [received[back - 1][0] for back in range(REACH - 1, 0, -1)] + [soft_keys], 0
    )
    value_window = jnp.concatenate(
        [received[back - 1][1] for back in range(REACH - 1, 0, -1)] + [soft_values], 0
    )
    query_place = jnp.arange(tokens, dtype=jnp.int32)
    key_place = jnp.arange(REACH * tokens, dtype=jnp.int32) - (REACH - 1) * tokens
    visible = (key_labels[None, :] == own_labels[:, None]) & (
        key_place[None, :] <= query_place[:, None]
    )
    soft_scores = (
        jnp.einsum("thd,uhd->htu", soft_queries, key_window, preferred_element_type=jnp.float32)
        * scale
    )
    soft_scores = jnp.where(visible[None], soft_scores, -jnp.inf)
    top = jnp.max(soft_scores, axis=-1)
    expo = jnp.exp(soft_scores - top[..., None])
    total = jnp.sum(expo, axis=-1)
    probs = expo / total[..., None]
    probs_half = probs.astype(jnp.bfloat16)
    attended = jnp.einsum(
        "htu,uhd->thd", probs_half, value_window, preferred_element_type=jnp.float32
    )
    delta = jnp.sum(as_float(soft_grads) * attended, axis=-1)
    grad_scores = score_grads(probs, soft_grads, value_window, delta)
    soft_query_grad = (
        jnp.einsum("htu,uhd->thd", grad_scores, key_window, preferred_element_type=jnp.float32)
        * scale
    )
    key_terms = (
        jnp.einsum("htu,thd->uhd", grad_scores, soft_queries, preferred_element_type=jnp.float32)
        * scale
    )
    value_terms = jnp.einsum(
        "htu,thd->uhd", probs_half, soft_grads, preferred_element_type=jnp.float32
    )
    soft_key_grad = key_terms[(REACH - 1) * tokens :]
    soft_value_grad = value_terms[(REACH - 1) * tokens :]
    items = {}
    for back in range(1, REACH):
        lower = (REACH - 1 - back) * tokens
        chain = jnp.prod(behind[REACH - back : REACH - 1], axis=0)
        items[back] = packed(
            key_terms[lower : lower + tokens],
            value_terms[lower : lower + tokens],
            chain[:, None, None] * back_summary,
        )
    size = items[1].shape[0]

    def wire(value):
        return value.astype(jnp.bfloat16)

    first = as_float(shifted(wire(jnp.concatenate([items[5], items[3], items[1]])), "seq", -1))
    second = as_float(
        shifted(
            wire(jnp.concatenate([items[2] + first[size : 2 * size], items[4] + first[:size]])),
            "seq",
            -2,
        )
    )
    third = as_float(shifted(wire(second[size:]), "seq", -2))
    total = first[2 * size :] + second[:size] + third
    got_key, got_value, reverse_in = unpacked(total, (kv_shape, kv_shape, state_shape))
    soft_key_grad = soft_key_grad + got_key
    soft_value_grad = soft_value_grad + got_value
    lin_key_grad = lin_key_grad + (
        jnp.einsum("she,hde->shd", as_float(values), reverse_in, precision=HIGH_PRECISION)
        * leave.T[:, :, None]
    )
    lin_value_grad = lin_value_grad + (
        jnp.einsum("shd,hde->she", as_float(keys), reverse_in, precision=HIGH_PRECISION)
        * leave.T[:, :, None]
    )

    def merge_heads(array):
        return with_layout_constraint(
            array.reshape(tokens, heads * HD).astype(jnp.bfloat16), Layout(major_to_minor=(0, 1))
        )

    return (
        merge_heads(lin_query_grad),
        merge_heads(lin_key_grad),
        merge_heads(lin_value_grad),
        merge_heads(soft_query_grad),
        merge_heads(soft_key_grad),
        merge_heads(soft_value_grad),
    )


def split_mesh(mesh):
    count = mesh.shape["tp"]
    inner = math.isqrt(count)
    if inner * inner != count:
        inner = 1
    devices = mesh.devices.reshape(mesh.shape["seq"], count // inner, inner)
    return jax.sharding.Mesh(devices, ("seq",) + TP)


def solution(mesh):
    return jax.shard_map(
        body,
        mesh=split_mesh(mesh),
        in_specs=(
            P("seq", TP),
            P("seq", TP),
            P("seq", TP),
            P(TP),
            P(TP),
            P("seq", TP),
            P("seq", TP),
            P("seq", TP),
            P("seq", TP),
            P("seq", TP),
            P(),
        ),
        out_specs=(
            P("seq", TP),
            P("seq", TP),
            P("seq", TP),
            P("seq", TP),
            P("seq", TP),
            P("seq", TP),
        ),
        check_vma=False,
    )
```

```python
import math

import jax
import jax.numpy as jnp
from jax import lax
from jax.experimental.layout import Layout, with_layout_constraint
from jax.sharding import PartitionSpec as P

HD = 128
BLK = 128
REACH = 6


HIGH_PRECISION = lax.Precision.HIGHEST
NORM_EPS = 1e-06
TP = ("tp_outer", "tp_inner")


def shifted(value, axis, steps):
    count = lax.axis_size(axis)
    first, last = (max(0, -steps), min(count, count - steps))
    return lax.ppermute(value, axis, [(source, source + steps) for source in range(first, last)])


def tp_sum(value, axes):
    for axis in reversed(axes):
        value = jnp.sum(lax.all_gather(value, axis), axis=0)
    return value


def packed(*parts):
    return jnp.concatenate([part.reshape(-1) for part in parts])


def unpacked(flat, shapes):
    out, at = [], 0
    for shape in shapes:
        size = math.prod(shape)
        out.append(flat[at : at + size].reshape(shape))
        at += size
    return out


def as_float(array):
    return array.astype(jnp.float32)


def decay_matrix(labels, decay_rate):
    place = jnp.arange(labels.shape[0], dtype=jnp.int32)
    distance = as_float(place[:, None] - place[None, :])
    visible = (labels[:, None] == labels[None, :]) & (distance >= 0)
    return jnp.where(
        visible[None], jnp.exp(-decay_rate[:, None, None] * jnp.maximum(distance, 0.0)[None]), 0.0
    )


def entry_weights(mask, decay_rate):
    place = as_float(jnp.arange(mask.shape[0], dtype=jnp.int32))
    return jnp.where(mask[None, :], jnp.exp(-decay_rate[:, None] * place[None, :]), 0.0)


def exit_weights(mask, decay_rate):
    count = mask.shape[0]
    place = as_float(jnp.arange(count, dtype=jnp.int32))
    return jnp.where(
        mask[None, :],
        jnp.exp(-decay_rate[:, None] * (count - 1 - place)[None, :]),
        0.0,
    )


def forward_summary(keys, values, mask, decay_rate):
    count = mask.shape[0]
    place = as_float(jnp.arange(count, dtype=jnp.int32))
    weight = jnp.where(
        mask[None, :],
        jnp.exp(-decay_rate[:, None] * (count - place)[None, :]),
        0.0,
    )
    return jnp.einsum(
        "thd,the->hde",
        as_float(keys) * weight.T[:, :, None],
        as_float(values),
        precision=HIGH_PRECISION,
    )


def backward_summary(queries, grads, mask, decay_rate):
    count = mask.shape[0]
    place = as_float(jnp.arange(count, dtype=jnp.int32))
    weight = jnp.where(
        mask[None, :],
        jnp.exp(-decay_rate[:, None] * (place + 1.0)[None, :]),
        0.0,
    )
    return jnp.einsum(
        "thd,the->hde",
        as_float(queries) * weight.T[:, :, None],
        as_float(grads),
        precision=HIGH_PRECISION,
    )


def score_grads(probs, grads, value_part, delta):
    grad_probs = jnp.einsum("thd,uhd->htu", grads, value_part, preferred_element_type=jnp.float32)
    return (probs * (grad_probs - delta.T[:, :, None])).astype(jnp.bfloat16)


def body(
    lin_query,
    lin_key,
    lin_value,
    decay_rate,
    norm_gain,
    lin_grad,
    soft_query,
    soft_key,
    soft_value,
    soft_grad,
    segments,
):
    tokens = lin_query.shape[0]
    heads = lin_query.shape[1] // HD
    scale = 1.0 / math.sqrt(HD)
    device = lax.axis_index("seq")
    blocks_each = tokens // BLK
    pad_blocks = REACH * blocks_each
    padded = jnp.concatenate(
        [jnp.full((pad_blocks,), -1, jnp.int32), segments, jnp.full((pad_blocks,), -2, jnp.int32)]
    )
    window_blocks = lax.dynamic_slice_in_dim(
        padded, device * blocks_each, (2 * REACH + 1) * blocks_each
    )
    window_labels = lax.optimization_barrier(
        jnp.broadcast_to(window_blocks[:, None], (window_blocks.shape[0], BLK)).reshape(-1)
    )
    own_labels = window_labels[REACH * tokens : (REACH + 1) * tokens]
    key_labels = window_labels[tokens : (REACH + 1) * tokens]

    def split_heads(array):
        return array.reshape(tokens, heads, HD)

    queries = split_heads(lin_query)
    keys = split_heads(lin_key)
    values = split_heads(lin_value)
    soft_queries = split_heads(soft_query)
    soft_keys = split_heads(soft_key)
    soft_values = split_heads(soft_value)
    soft_grads = split_heads(soft_grad)
    span = 2 * REACH + 1
    firsts = window_blocks[::blocks_each]
    lasts = window_blocks[blocks_each - 1 :: blocks_each]
    if blocks_each == 1:
        same_first = same_last = jnp.ones((tokens,), bool)
        same_next = own_labels == window_labels[(REACH + 1) * tokens : (REACH + 2) * tokens]
        same_prev = own_labels == window_labels[(REACH - 1) * tokens : REACH * tokens]
    else:
        same_first = own_labels == own_labels[:1]
        same_last = own_labels == own_labels[-1:]
        same_next = same_last & (lasts[REACH : REACH + 1] == firsts[REACH + 1 : REACH + 2])
        same_prev = same_first & (firsts[REACH : REACH + 1] == lasts[REACH - 1 : REACH])
    summary = forward_summary(keys, values, same_next, decay_rate)
    full_decay = jnp.exp(-decay_rate * tokens)
    ahead = jnp.where((firsts[:-1] == firsts[1:])[:, None], full_decay[None, :], 0.0)
    behind = jnp.where(
        ((firsts[1:] == lasts[:-1]) & (firsts[1:] == lasts[1:]))[:, None], full_decay[None, :], 0.0
    )
    kv_shape = soft_keys.shape
    state_shape = summary.shape
    unit = packed(soft_keys, soft_values, summary.astype(jnp.bfloat16))
    size = unit.shape[0]
    two_back = shifted(unit, "seq", 2)
    four_back = shifted(two_back, "seq", 2)
    odd_back = shifted(jnp.concatenate([unit, two_back]), "seq", 1)
    five_back = shifted(two_back, "seq", 3)
    arrived = {
        1: odd_back[:size],
        2: two_back,
        3: odd_back[size:],
        4: four_back,
        5: five_back,
    }
    received = []
    state_in = jnp.zeros_like(summary)
    for back in range(1, REACH):
        got_key, got_value, got_state = unpacked(arrived[back], (kv_shape, kv_shape, state_shape))
        received.append((got_key, got_value))
        chain = jnp.prod(ahead[REACH - back + 1 : REACH], axis=0)
        state_in = state_in + chain[:, None, None] * as_float(got_state)
    decay = decay_matrix(own_labels, decay_rate)
    scores = jnp.einsum("thd,shd->hts", queries, keys, preferred_element_type=jnp.float32)
    weights = (decay * scores).astype(jnp.bfloat16)
    entry = entry_weights(same_first, decay_rate)
    leave = exit_weights(same_last, decay_rate)
    inner = jnp.einsum("hts,shd->thd", weights, values, preferred_element_type=jnp.float32)
    carried = jnp.einsum("thd,hde->the", as_float(queries), state_in, precision=HIGH_PRECISION)
    lin_out = inner + carried * entry.T[:, :, None]
    flat = lin_out.reshape(tokens, heads * HD)
    scaled_grad = norm_gain[None, :] * as_float(lin_grad)
    sums = tp_sum(jnp.stack([jnp.sum(flat * flat, axis=1), jnp.sum(flat * scaled_grad, axis=1)]), TP)
    width = lax.axis_size(TP) * heads * HD
    inverse = lax.rsqrt(sums[0] / width + NORM_EPS)
    cross = sums[1] / width
    norm_grad = (inverse[:, None] * scaled_grad - flat * (inverse**3 * cross)[:, None]).astype(
        jnp.bfloat16
    )
    grad_heads = split_heads(norm_grad)
    back_summary = backward_summary(queries, grad_heads, same_prev, decay_rate)
    back_state = back_summary.astype(jnp.bfloat16)
    grad_scores_lin = jnp.einsum(
        "thd,shd->hts", grad_heads, values, preferred_element_type=jnp.float32
    )
    grad_weights = (decay * grad_scores_lin).astype(jnp.bfloat16)
    lin_query_grad = jnp.einsum(
        "hts,shd->thd", grad_weights, keys, preferred_element_type=jnp.float32
    )
    lin_query_grad = (
        lin_query_grad
        + jnp.einsum("the,hde->thd", as_float(grad_heads), state_in, precision=HIGH_PRECISION)
        * entry.T[:, :, None]
    )
    lin_key_grad = jnp.einsum(
        "hts,thd->shd", grad_weights, queries, preferred_element_type=jnp.float32
    )

    lin_value_grad = jnp.einsum(
        "hts,the->she", weights, grad_heads, preferred_element_type=jnp.float32
    )

    key_window = jnp.concatenate(
        [received[back - 1][0] for back in range(REACH - 1, 0, -1)] + [soft_keys], 0
    )
    value_window = jnp.concatenate(
        [received[back - 1][1] for back in range(REACH - 1, 0, -1)] + [soft_values], 0
    )
    query_place = jnp.arange(tokens, dtype=jnp.int32)
    key_place = jnp.arange(REACH * tokens, dtype=jnp.int32) - (REACH - 1) * tokens
    visible = (key_labels[None, :] == own_labels[:, None]) & (
        key_place[None, :] <= query_place[:, None]
    )
    soft_scores = (
        jnp.einsum("thd,uhd->htu", soft_queries, key_window, preferred_element_type=jnp.float32)
        * scale
    )
    soft_scores = jnp.where(visible[None], soft_scores, -jnp.inf)
    top = jnp.max(soft_scores, axis=-1)
    expo = jnp.exp(soft_scores - top[..., None])
    total = jnp.sum(expo, axis=-1)
    probs = expo / total[..., None]
    probs_half = probs.astype(jnp.bfloat16)
    attended = jnp.einsum(
        "htu,uhd->thd", probs_half, value_window, preferred_element_type=jnp.float32
    )
    delta = jnp.sum(as_float(soft_grads) * attended, axis=-1)
    grad_scores = score_grads(probs, soft_grads, value_window, delta)
    soft_query_grad = (
        jnp.einsum("htu,uhd->thd", grad_scores, key_window, preferred_element_type=jnp.float32)
        * scale
    )
    key_terms = (
        jnp.einsum("htu,thd->uhd", grad_scores, soft_queries, preferred_element_type=jnp.float32)
        * scale
    )
    value_terms = jnp.einsum(
        "htu,thd->uhd", probs_half, soft_grads, preferred_element_type=jnp.float32
    )
    soft_key_grad = key_terms[(REACH - 1) * tokens :]
    soft_value_grad = value_terms[(REACH - 1) * tokens :]
    soft_part = {}
    items = {}
    for back in range(1, REACH):
        lower = (REACH - 1 - back) * tokens
        chain = jnp.prod(behind[REACH - back : REACH - 1], axis=0)
        soft_part[back] = packed(key_terms[lower : lower + tokens], value_terms[lower : lower + tokens])
        items[back] = jnp.concatenate(
            [soft_part[back], (chain[:, None, None] * back_summary).reshape(-1)]
        )
    soft_size = soft_part[1].shape[0]
    size = items[1].shape[0]

    def wire(value):
        return value.astype(jnp.bfloat16)

    first = as_float(
        shifted(
            wire(
                jnp.concatenate(
                    [soft_part[5], soft_part[3], soft_part[1], back_summary.reshape(-1)]
                )
            ),
            "seq",
            -1,
        )
    )
    raw = first[3 * soft_size :].reshape(state_shape)

    def landed(slot, back):
        chain = jnp.prod(behind[REACH - back + 1 : REACH], axis=0)
        return jnp.concatenate(
            [
                first[slot * soft_size : (slot + 1) * soft_size],
                (chain[:, None, None] * raw).reshape(-1),
            ]
        )

    second = as_float(
        shifted(
            wire(jnp.concatenate([items[2] + landed(1, 3), items[4] + landed(0, 5)])),
            "seq",
            -2,
        )
    )
    third = as_float(shifted(wire(second[size:]), "seq", -2))
    total = landed(2, 1) + second[:size] + third
    got_key, got_value, reverse_in = unpacked(total, (kv_shape, kv_shape, state_shape))
    soft_key_grad = soft_key_grad + got_key
    soft_value_grad = soft_value_grad + got_value
    lin_key_grad = lin_key_grad + (
        jnp.einsum("she,hde->shd", as_float(values), reverse_in, precision=HIGH_PRECISION)
        * leave.T[:, :, None]
    )
    lin_value_grad = lin_value_grad + (
        jnp.einsum("shd,hde->she", as_float(keys), reverse_in, precision=HIGH_PRECISION)
        * leave.T[:, :, None]
    )

    def merge_heads(array):
        return with_layout_constraint(
            array.reshape(tokens, heads * HD).astype(jnp.bfloat16), Layout(major_to_minor=(0, 1))
        )

    return (
        merge_heads(lin_query_grad),
        merge_heads(lin_key_grad),
        merge_heads(lin_value_grad),
        merge_heads(soft_query_grad),
        merge_heads(soft_key_grad),
        merge_heads(soft_value_grad),
    )


def split_mesh(mesh):
    count = mesh.shape["tp"]
    inner = math.isqrt(count)
    if inner * inner != count:
        inner = 1
    devices = mesh.devices.reshape(mesh.shape["seq"], count // inner, inner)
    return jax.sharding.Mesh(devices, ("seq",) + TP)


def solution(mesh):
    return jax.shard_map(
        body,
        mesh=split_mesh(mesh),
        in_specs=(
            P("seq", TP),
            P("seq", TP),
            P("seq", TP),
            P(TP),
            P(TP),
            P("seq", TP),
            P("seq", TP),
            P("seq", TP),
            P("seq", TP),
            P("seq", TP),
            P(),
        ),
        out_specs=(
            P("seq", TP),
            P("seq", TP),
            P("seq", TP),
            P("seq", TP),
            P("seq", TP),
            P("seq", TP),
        ),
        check_vma=False,
    )
```
